32 devices in a mesh: win: 2 (over x), chan: 16 (over z, y, core).
Axes of the slice: x: 2, y: 2, z: 4, core: 2. Of those that a mesh axis runs over, the one named last changes fastest.
Arguments:
- waveform: bfloat16 [128, 1024], P('chan', 'win'), parts along dimension 1, may hold values from -60 to 60
- templates: bfloat16 [1024, 128, 128], P(None, 'chan'), may hold values from -6 to 6
- moveouts: int32 [1024, 128], P(None, 'chan'), may hold values from 0 to 127
- valid: int32 [128], P('chan'), may hold values 0 or 1
Outputs:
- best: float32 [512], P(('win', 'chan')), parts along dimension 0
The draws below stay inside these ranges and needn't reach their ends.
There are 2 independent parts, one for each index of `win`. The reference program is written for one: setup_inputs(seed, part) draws one part's arguments, and reference() takes and returns one part's arrays. A program takes and returns all parts, laid end to end along the dimension named above; an argument that names none is the same for every part. Nothing has to cross between parts.
All inputs are finite; a program needn't handle non-finite values. No bound on the sum of `valid` on one device may be relied on, other than what follows from the above.
Results may differ from the reference program's by a relative error of at most 0.0003.
Values sent between devices are 32-bit elements; how exact they have to be, the bound alone decides.
No kernel may reach another device: no remote copies, remote signals or barrier semaphores. Data moves between devices by JAX's collectives and lax.ppermute only.
A program may use at most 64 MiB of HBM per device.

```python
import math
import jax
import jax.numpy as jnp
from jax import lax

T_OUT = 256
K = 1024
S = 128
MAXSHIFT = 128
CH = 128
SPAN = 512


def draw_waveform(key, part):
    noise_key = jax.random.fold_in(key, 11)
    chan_key = jax.random.fold_in(key, 12)
    time_key = jax.random.fold_in(key, 13)
    channel = jnp.arange(CH, dtype=jnp.float32)
    ramp = jnp.exp(jnp.log(3.0) * channel / max(CH - 1, 1))
    spread = jnp.exp(jax.random.uniform(chan_key, (CH,), jnp.float32, 0.0, jnp.log(3.4)))
    amp = (ramp * spread)[:, None]
    envelope = jnp.exp(jax.random.uniform(time_key, (SPAN,), jnp.float32, 0.0, jnp.log(3.0)))[None, :]
    noise = jax.random.normal(noise_key, (CH, SPAN), jnp.float32)
    values = noise * amp * envelope
    return jnp.clip(values, -60.0, 60.0).astype(jnp.bfloat16)


def touch_ends(values, own_key, least, top_value):
    shape = values.shape
    spot = [jax.random.randint(jax.random.fold_in(own_key, axis), (), 0, shape[axis]) for axis in range(len(shape))]
    values = values.at[tuple(spot)].set(least)
    longest = shape.index(max(shape))
    spot[longest] = (spot[longest] + 1) % shape[longest]
    return values.at[tuple(spot)].set(top_value)


def block_levels(own_key, dims, pieces, smallest, top_value):
    loudness, own = 1.0, jax.random.fold_in(own_key, 6)
    for dim, blocks in pieces:
        steps = jnp.exp(jax.random.uniform(jax.random.fold_in(own, dim), (blocks,), jnp.float32, smallest / len(pieces), top_value / len(pieces)))
        loudness = loudness * jnp.repeat(steps, dims[dim] // blocks).reshape([-1 if axis == dim else 1 for axis in range(len(dims))])
    return loudness


def gaussian(own_key, dims, deviation, reach, cuts=(), held_as=jnp.bfloat16):
    values = deviation * jax.random.normal(own_key, dims, jnp.float32)
    if cuts:
        values = values * block_levels(own_key, dims, cuts, -0.22, 0.18)
    return jnp.clip(values, -reach, reach).astype(held_as)


def setup_inputs(seed: int = 0, part: int = 0) -> dict:
    arg_keys = jax.random.split(jax.random.key(seed), 5)
    part_splits = jax.random.split(jax.random.fold_in(arg_keys[4], part), 5)
    waveform = draw_waveform(jax.random.fold_in(jax.random.fold_in(arg_keys[4], part), 71), part)
    templates = gaussian(arg_keys[1], (K, CH, S), 1.0, 6.0, ((1, 16),))
    moveouts = touch_ends(jax.random.randint(arg_keys[2], (K, CH), 0, MAXSHIFT), jax.random.fold_in(arg_keys[2], 1), 0, MAXSHIFT - 1).astype(jnp.int32)
    valid = touch_ends((jax.random.randint(arg_keys[3], (CH,), 0, 8) < 7).astype(jnp.int32), jax.random.fold_in(arg_keys[3], 1), 0, 1)
    return {"waveform": waveform, "templates": templates, "moveouts": moveouts, "valid": valid}


def place_templates(templates, moveouts):
    width = S + MAXSHIFT
    position = jnp.arange(width, dtype=jnp.int32)[None, None, :] - moveouts[:, :, None].astype(jnp.int32)
    inside = (position >= 0) & (position < S)
    values = jnp.take_along_axis(templates, jnp.clip(position, 0, S - 1).astype(jnp.int32), axis=2)
    return jnp.where(inside, values, jnp.zeros_like(values))

def reference(waveform, templates, moveouts, valid):
    width = S + MAXSHIFT
    masked = jnp.where(valid[:, None] == 1, waveform, jnp.zeros_like(waveform))
    index = jnp.arange(T_OUT, dtype=jnp.int32)[:, None] + jnp.arange(width, dtype=jnp.int32)[None, :]
    block = math.gcd(CH, 32)

    def add_block(total, number):
        first = (number * block).astype(jnp.int32)
        rows = lax.dynamic_slice_in_dim(masked, first, block, 0)
        traces = lax.dynamic_slice_in_dim(templates, first, block, 1)
        delays = lax.dynamic_slice_in_dim(moveouts, first, block, 1)
        placed = place_templates(traces, delays)
        hankel = rows[:, index]
        term = lax.dot_general(hankel, placed, (((0, 2), (1, 2)), ((), ())), preferred_element_type=jnp.float32)
        return (total + term, None)
    corr, _ = lax.scan(add_block, jnp.zeros((T_OUT, K), jnp.float32), jnp.arange(CH // block, dtype=jnp.int32))
    squares = lax.optimization_barrier(jnp.sum(masked.astype(jnp.float32) ** 2, axis=0))
    energy = lax.optimization_barrier(jnp.sum(squares[index], axis=1))
    return lax.optimization_barrier(jnp.max(corr / jnp.sqrt(energy + 1e-06)[:, None], axis=1))
```

```python
import jax
import jax.numpy as jnp
from jax import lax
from jax.experimental import pallas as pl
from jax.experimental.pallas import tpu as pltpu
from jax.sharding import PartitionSpec as P

MAXSHIFT = 128
LANES = 128


def place_block(tr, mrow):
    rows, cols = tr.shape
    width = rows + MAXSHIFT
    fine = jnp.concatenate([jnp.zeros((8, cols), tr.dtype), tr], axis=0)
    for level in range(3):
        amount = 1 << level
        moved = pltpu.roll(fine, fine.shape[0] - amount, 0)
        fine = jnp.where((mrow >> level) & 1 == 1, moved, fine)
    x = jnp.concatenate([jnp.zeros((width - fine.shape[0], cols), tr.dtype), fine], axis=0)
    for level in range(3, (MAXSHIFT - 1).bit_length()):
        amount = 1 << level
        moved = jnp.concatenate([x[amount:], jnp.zeros((amount, cols), x.dtype)], axis=0)
        x = jnp.where((mrow >> level) & 1 == 1, moved, x)
    return x


def corr_kernel(wr_ref, t_ref, m_ref, out_ref, h_scr, p_scr):
    nc, span = wr_ref.shape
    k_all, _, length = t_ref.shape
    width = length + MAXSHIFT
    out_len = span - width
    for c in range(nc):
        row = wr_ref[pl.ds(c, 1), :]
        a = pltpu.roll(jnp.broadcast_to(row, (out_len, span)), 0, 1, stride=1, stride_axis=0)
        h_scr[:, c * width:(c + 1) * width] = a[:, span - width:].astype(jnp.bfloat16)
    wr = wr_ref[...]
    q = jnp.sum(wr * wr, axis=0, keepdims=True)
    aq = pltpu.roll(jnp.broadcast_to(q, (out_len, span)), 0, 1, stride=1, stride_axis=0)
    energy = jnp.sum(aq[:, span - width:], axis=1, keepdims=True)
    out_ref[:, k_all:] = jnp.broadcast_to(energy, (out_len, out_ref.shape[1] - k_all))

    ri = lax.broadcasted_iota(jnp.int32, (length, length), 0)
    ci = lax.broadcasted_iota(jnp.int32, (length, length), 1)
    flip = jnp.where(ri + ci == length - 1, 1.0, 0.0).astype(jnp.bfloat16)
    for c in range(nc):
        def body(kc, carry):
            k0 = pl.multiple_of(kc * LANES, LANES)
            tk = t_ref[pl.ds(k0, LANES), c, :]
            tr = lax.dot_general(
                flip, tk, (((1,), (1,)), ((), ())), preferred_element_type=jnp.float32
            )
            mrow = m_ref[pl.ds(c, 1), pl.ds(k0, LANES)]
            x = place_block(tr, mrow)
            p_scr[pl.ds(c * width, width), pl.ds(k0, LANES)] = x.astype(jnp.bfloat16)
            return carry

        lax.fori_loop(0, k_all // LANES, body, 0)
    step = 256
    for n0 in range(0, k_all, step):
        out_ref[:, n0:n0 + step] = jnp.dot(
            h_scr[...], p_scr[:, n0:n0 + step], preferred_element_type=jnp.float32
        )


def local_corr(wr, templates, mt):
    nc, span = wr.shape
    k_all, _, length = templates.shape
    width = length + MAXSHIFT
    out_len = span - width
    return pl.pallas_call(
        corr_kernel,
        out_shape=jax.ShapeDtypeStruct((out_len, k_all + LANES), jnp.float32),
        in_specs=[pl.BlockSpec(memory_space=pltpu.VMEM)] * 3,
        out_specs=pl.BlockSpec(memory_space=pltpu.VMEM),
        scratch_shapes=[
            pltpu.VMEM((out_len, nc * width), jnp.bfloat16),
            pltpu.VMEM((nc * width, k_all), jnp.bfloat16),
        ],
        compiler_params=pltpu.CompilerParams(vmem_limit_bytes=48 * 1024 * 1024),
        cost_estimate=pl.CostEstimate(
            flops=2 * out_len * nc * width * k_all,
            bytes_accessed=templates.size * 2 + out_len * (k_all + LANES) * 4,
            transcendentals=0,
        ),
    )(wr, templates, mt)


def on_device(waveform, templates, moveouts, valid):
    k_all = templates.shape[0]
    masked = jnp.where(valid[:, None] == 1, waveform, jnp.zeros_like(waveform))
    wr = jnp.flip(masked, axis=1).astype(jnp.float32)
    both = local_corr(wr, templates, moveouts.T)
    summed = lax.psum_scatter(both, "chan", scatter_dimension=0, tiled=True)
    scale = jnp.sqrt(summed[:, k_all] + 1e-06)
    best = jnp.max(summed[:, :k_all] / scale[:, None], axis=1)
    return best


def solution(mesh):
    placed = (P("chan", "win"), P(None, "chan", None), P(None, "chan"), P("chan"))
    return jax.shard_map(
        on_device, mesh=mesh, in_specs=placed, out_specs=P(("win", "chan")), check_vma=False
    )
```

```python
import jax
import jax.numpy as jnp
from jax import lax
from jax.experimental import pallas as pl
from jax.experimental.pallas import tpu as pltpu
from jax.sharding import PartitionSpec as P

MAXSHIFT = 128
LANES = 128


def place_block(tr, mrow):
    rows, cols = tr.shape
    width = rows + MAXSHIFT
    fine = jnp.concatenate([jnp.zeros((8, cols), tr.dtype), tr], axis=0)
    for level in range(3):
        amount = 1 << level
        moved = pltpu.roll(fine, fine.shape[0] - amount, 0)
        fine = jnp.where((mrow >> level) & 1 == 1, moved, fine)
    x = jnp.concatenate([jnp.zeros((width - fine.shape[0], cols), tr.dtype), fine], axis=0)
    for level in range(3, (MAXSHIFT - 1).bit_length()):
        amount = 1 << level
        moved = jnp.concatenate([x[amount:], jnp.zeros((amount, cols), x.dtype)], axis=0)
        x = jnp.where((mrow >> level) & 1 == 1, moved, x)
    return x


def corr_kernel(wr_ref, t_ref, m_ref, out_ref, h_scr, p_scr):
    nc, span = wr_ref.shape
    k_all, _, length = t_ref.shape
    width = length + MAXSHIFT
    out_len = span - width
    for c in range(nc):
        row = wr_ref[pl.ds(c, 1), :]
        a = pltpu.roll(jnp.broadcast_to(row, (out_len, span)), 0, 1, stride=1, stride_axis=0)
        h_scr[:, c * width:(c + 1) * width] = a[:, span - width:].astype(jnp.bfloat16)
    wr = wr_ref[...]
    q = jnp.sum(wr * wr, axis=0, keepdims=True)
    aq = pltpu.roll(jnp.broadcast_to(q, (out_len, span)), 0, 1, stride=1, stride_axis=0)
    energy = jnp.sum(aq[:, span - width:], axis=1, keepdims=True)
    out_ref[:, k_all:] = jnp.broadcast_to(energy, (out_len, out_ref.shape[1] - k_all))

    ri = lax.broadcasted_iota(jnp.int32, (length, length), 0)
    ci = lax.broadcasted_iota(jnp.int32, (length, length), 1)
    flip = jnp.where(ri + ci == length - 1, 1.0, 0.0).astype(jnp.bfloat16)
    for c in range(nc):
        def body(kc, carry):
            k0 = pl.multiple_of(kc * LANES, LANES)
            tk = t_ref[pl.ds(k0, LANES), c, :]
            tr = lax.dot_general(
                flip, tk, (((1,), (1,)), ((), ())), preferred_element_type=jnp.float32
            )
            mrow = m_ref[pl.ds(c, 1), pl.ds(k0, LANES)]
            x = place_block(tr, mrow)
            p_scr[pl.ds(c * width, width), pl.ds(k0, LANES)] = x.astype(jnp.bfloat16)
            return carry

        lax.fori_loop(0, k_all // LANES, body, 0)
    step = 256
    for n0 in range(0, k_all, step):
        out_ref[:, n0:n0 + step] = jnp.dot(
            h_scr[...], p_scr[:, n0:n0 + step], preferred_element_type=jnp.float32
        )


def local_corr(wr, templates, mt):
    nc, span = wr.shape
    k_all, _, length = templates.shape
    width = length + MAXSHIFT
    out_len = span - width
    return pl.pallas_call(
        corr_kernel,
        out_shape=jax.ShapeDtypeStruct((out_len, k_all + LANES), jnp.float32),
        in_specs=[pl.BlockSpec(memory_space=pltpu.VMEM)] * 3,
        out_specs=pl.BlockSpec(memory_space=pltpu.VMEM),
        scratch_shapes=[
            pltpu.VMEM((out_len, nc * width), jnp.bfloat16),
            pltpu.VMEM((nc * width, k_all), jnp.bfloat16),
        ],
        compiler_params=pltpu.CompilerParams(vmem_limit_bytes=48 * 1024 * 1024),
        cost_estimate=pl.CostEstimate(
            flops=2 * out_len * nc * width * k_all,
            bytes_accessed=templates.size * 2 + out_len * (k_all + LANES) * 4,
            transcendentals=0,
        ),
    )(wr, templates, mt)


def halving_reduce_scatter(x, axis):
    count = lax.axis_size(axis)
    if count & (count - 1):
        return lax.psum_scatter(x, axis, scatter_dimension=0, tiled=True)
    me = lax.axis_index(axis)
    rows, cols = x.shape
    blocks = x.reshape(count, rows // count, cols)
    bit = 0
    while (1 << bit) < count:
        mine = (me >> bit) & 1
        pairs = blocks.reshape(-1, 2, rows // count, cols)
        keep = lax.dynamic_index_in_dim(pairs, mine, axis=1, keepdims=False)
        send = lax.dynamic_index_in_dim(pairs, 1 - mine, axis=1, keepdims=False)
        perm = [(j, j ^ (1 << bit)) for j in range(count)]
        blocks = keep + lax.ppermute(send, axis, perm)
        bit += 1
    return blocks.reshape(rows // count, cols)


def on_device(waveform, templates, moveouts, valid):
    k_all = templates.shape[0]
    masked = jnp.where(valid[:, None] == 1, waveform, jnp.zeros_like(waveform))
    wr = jnp.flip(masked, axis=1).astype(jnp.float32)
    both = local_corr(wr, templates, moveouts.T)
    summed = halving_reduce_scatter(both, "chan")
    scale = jnp.sqrt(summed[:, k_all] + 1e-06)
    best = jnp.max(summed[:, :k_all] / scale[:, None], axis=1)
    return best


def solution(mesh):
    placed = (P("chan", "win"), P(None, "chan", None), P(None, "chan"), P("chan"))
    return jax.shard_map(
        on_device, mesh=mesh, in_specs=placed, out_specs=P(("win", "chan")), check_vma=False
    )
```

```python
import jax
import jax.numpy as jnp
from jax import lax
from jax.experimental import pallas as pl
from jax.experimental.pallas import tpu as pltpu
from jax.sharding import PartitionSpec as P

MAXSHIFT = 128
LANES = 128


def place_block(tr, mrow):
    rows, cols = tr.shape
    width = rows + MAXSHIFT
    fine = jnp.concatenate([tr, jnp.zeros((8, cols), tr.dtype)], axis=0)
    for level in range(3):
        amount = 1 << level
        moved = pltpu.roll(fine, amount, 0)
        fine = jnp.where((mrow >> level) & 1 == 1, moved, fine)
    x = jnp.concatenate([fine, jnp.zeros((width - fine.shape[0], cols), tr.dtype)], axis=0)
    for level in range(3, (MAXSHIFT - 1).bit_length()):
        amount = 1 << level
        moved = jnp.concatenate([jnp.zeros((amount, cols), x.dtype), x[: width - amount]], axis=0)
        x = jnp.where((mrow >> level) & 1 == 1, moved, x)
    return x


def corr_kernel(valid_ref, w_ref, t_hbm, m_ref, out_ref, h_scr, p_scr, t_buf, sems):
    nc, span = w_ref.shape
    k_all = t_hbm.shape[0]
    length = t_hbm.shape[1] // nc
    width = length + MAXSHIFT
    out_len = span - width
    copies = []
    for c in range(nc):
        copy = pltpu.make_async_copy(
            t_hbm.at[:, pl.ds(c * length, length)], t_buf.at[c], sems.at[c]
        )
        copy.start()
        copies.append(copy)
    q = jnp.zeros((1, span), jnp.float32)
    for c in range(nc):
        row = w_ref[pl.ds(c, 1), :].astype(jnp.float32)
        row = jnp.where(valid_ref[c] == 1, row, 0.0)
        q = q + row * row
        a = pltpu.roll(jnp.broadcast_to(row, (out_len, span)), 1, 1, stride=1, stride_axis=0)
        h_scr[:, c * width:(c + 1) * width] = a[:, span - width:].astype(jnp.bfloat16)
    aq = pltpu.roll(jnp.broadcast_to(q, (out_len, span)), 1, 1, stride=1, stride_axis=0)
    energy = jnp.sum(aq[:, span - width:], axis=1, keepdims=True)
    out_ref[:, k_all:] = jnp.broadcast_to(energy, (out_len, out_ref.shape[1] - k_all))

    ri = lax.broadcasted_iota(jnp.int32, (length, length), 0)
    ci = lax.broadcasted_iota(jnp.int32, (length, length), 1)
    eye = jnp.where(ri == ci, 1.0, 0.0).astype(jnp.bfloat16)
    for c in range(nc):
        copies[c].wait()

        def body(kc, carry):
            k0 = pl.multiple_of(kc * LANES, LANES)
            tk = t_buf[c, pl.ds(k0, LANES), :]
            tr = lax.dot_general(
                eye, tk, (((1,), (1,)), ((), ())), preferred_element_type=jnp.float32
            )
            mrow = m_ref[pl.ds(c, 1), pl.ds(k0, LANES)]
            x = place_block(tr, mrow)
            p_scr[pl.ds(c * width, width), pl.ds(k0, LANES)] = x.astype(jnp.bfloat16)
            return carry

        lax.fori_loop(0, k_all // LANES, body, 0)
    step = 256
    for n0 in range(0, k_all, step):
        out_ref[:, n0:n0 + step] = jnp.dot(
            h_scr[...], p_scr[:, n0:n0 + step], preferred_element_type=jnp.float32
        )


def local_corr(valid, waveform, templates2, mt):
    nc, span = waveform.shape
    k_all = templates2.shape[0]
    length = templates2.shape[1] // nc
    width = length + MAXSHIFT
    out_len = span - width
    return pl.pallas_call(
        corr_kernel,
        out_shape=jax.ShapeDtypeStruct((out_len, k_all + LANES), jnp.float32),
        in_specs=[
            pl.BlockSpec(memory_space=pltpu.SMEM),
            pl.BlockSpec(memory_space=pltpu.VMEM),
            pl.BlockSpec(memory_space=pl.ANY),
            pl.BlockSpec(memory_space=pltpu.VMEM),
        ],
        out_specs=pl.BlockSpec(memory_space=pltpu.VMEM),
        scratch_shapes=[
            pltpu.VMEM((out_len, nc * width), jnp.bfloat16),
            pltpu.VMEM((nc * width, k_all), jnp.bfloat16),
            pltpu.VMEM((nc, k_all, length), jnp.bfloat16),
            pltpu.SemaphoreType.DMA((nc,)),
        ],
        compiler_params=pltpu.CompilerParams(vmem_limit_bytes=48 * 1024 * 1024),
        cost_estimate=pl.CostEstimate(
            flops=2 * out_len * nc * width * k_all,
            bytes_accessed=templates2.size * 2 + out_len * (k_all + LANES) * 4,
            transcendentals=0,
        ),
    )(valid, waveform, templates2, mt)


def halving_reduce_scatter(x, axis):
    count = lax.axis_size(axis)
    if count & (count - 1):
        natural = lax.psum_scatter(jnp.flip(x, 0), axis, scatter_dimension=0, tiled=True)
        return jnp.flip(natural, 0)
    me = count - 1 - lax.axis_index(axis)
    rows, cols = x.shape
    blocks = x.reshape(count, rows // count, cols)
    bit = 0
    while (1 << bit) < count:
        mine = (me >> bit) & 1
        pairs = blocks.reshape(-1, 2, rows // count, cols)
        keep = lax.dynamic_index_in_dim(pairs, mine, axis=1, keepdims=False)
        send = lax.dynamic_index_in_dim(pairs, 1 - mine, axis=1, keepdims=False)
        perm = [(j, j ^ (1 << bit)) for j in range(count)]
        blocks = keep + lax.ppermute(send, axis, perm)
        bit += 1
    return blocks.reshape(rows // count, cols)


def on_device(waveform, templates, moveouts, valid):
    k_all = templates.shape[0]
    templates2 = templates.reshape(k_all, -1)
    both = local_corr(valid, waveform, templates2, moveouts.T)
    summed = jnp.flip(halving_reduce_scatter(both, "chan"), axis=0)
    scale = jnp.sqrt(summed[:, k_all] + 1e-06)
    best = jnp.max(summed[:, :k_all] / scale[:, None], axis=1)
    return best


def solution(mesh):
    placed = (P("chan", "win"), P(None, "chan", None), P(None, "chan"), P("chan"))
    return jax.shard_map(
        on_device, mesh=mesh, in_specs=placed, out_specs=P(("win", "chan")), check_vma=False
    )
```

```python
import jax
import jax.numpy as jnp
from jax import lax
from jax.experimental import pallas as pl
from jax.experimental.pallas import tpu as pltpu
from jax.sharding import PartitionSpec as P

MAXSHIFT = 128
LANES = 128


def place_block(tr, mrow):
    rows, cols = tr.shape
    width = rows + MAXSHIFT
    fine = jnp.concatenate([tr, jnp.zeros((8, cols), tr.dtype)], axis=0)
    for level in range(3):
        amount = 1 << level
        moved = pltpu.roll(fine, amount, 0)
        fine = jnp.where((mrow >> level) & 1 == 1, moved, fine)
    x = jnp.concatenate([fine, jnp.zeros((width - fine.shape[0], cols), tr.dtype)], axis=0)
    for level in range(3, (MAXSHIFT - 1).bit_length()):
        amount = 1 << level
        moved = jnp.concatenate([jnp.zeros((amount, cols), x.dtype), x[: width - amount]], axis=0)
        x = jnp.where((mrow >> level) & 1 == 1, moved, x)
    return x


def corr_kernel(valid_ref, w_ref, t_hbm, m_ref, out_ref, h_scr, p_scr, t_buf, sems):
    nc, span = w_ref.shape
    k_all = t_hbm.shape[0]
    length = t_hbm.shape[1] // nc
    width = length + MAXSHIFT
    out_len = span - width
    copies = []
    for c in range(nc):
        copy = pltpu.make_async_copy(
            t_hbm.at[:, pl.ds(c * length, length)], t_buf.at[c], sems.at[c]
        )
        copy.start()
        copies.append(copy)
    q = jnp.zeros((1, span), jnp.float32)
    for c in range(nc):
        row = w_ref[pl.ds(c, 1), :].astype(jnp.float32)
        row = jnp.where(valid_ref[c] == 1, row, 0.0)
        q = q + row * row
        a = pltpu.roll(jnp.broadcast_to(row, (out_len, span)), 1, 1, stride=1, stride_axis=0)
        h_scr[:, c * width:(c + 1) * width] = a[:, span - width:].astype(jnp.bfloat16)
    aq = pltpu.roll(jnp.broadcast_to(q, (out_len, span)), 1, 1, stride=1, stride_axis=0)
    energy = jnp.sum(aq[:, span - width:], axis=1, keepdims=True)
    out_ref[:, k_all:] = jnp.broadcast_to(energy, (out_len, out_ref.shape[1] - k_all))

    ri = lax.broadcasted_iota(jnp.int32, (length, length), 0)
    ci = lax.broadcasted_iota(jnp.int32, (length, length), 1)
    eye = jnp.where(ri == ci, 1.0, 0.0).astype(jnp.bfloat16)
    for c in range(nc):
        copies[c].wait()

        def body(kc, carry):
            k0 = pl.multiple_of(kc * LANES, LANES)
            tk = t_buf[c, pl.ds(k0, LANES), :]
            tr = lax.dot_general(
                eye, tk, (((1,), (1,)), ((), ())), preferred_element_type=jnp.float32
            )
            mrow = m_ref[pl.ds(c, 1), pl.ds(k0, LANES)]
            x = place_block(tr, mrow)
            p_scr[pl.ds(c * width, width), pl.ds(k0, LANES)] = x.astype(jnp.bfloat16)
            return carry

        lax.fori_loop(0, k_all // LANES, body, 0)
    step = 256
    for n0 in range(0, k_all, step):
        out_ref[:, n0:n0 + step] = jnp.dot(
            h_scr[...], p_scr[:, n0:n0 + step], preferred_element_type=jnp.float32
        )


def local_corr(valid, waveform, templates2, mt):
    nc, span = waveform.shape
    k_all = templates2.shape[0]
    length = templates2.shape[1] // nc
    width = length + MAXSHIFT
    out_len = span - width
    return pl.pallas_call(
        corr_kernel,
        out_shape=jax.ShapeDtypeStruct((out_len, k_all + LANES), jnp.float32),
        in_specs=[
            pl.BlockSpec(memory_space=pltpu.SMEM),
            pl.BlockSpec(memory_space=pltpu.VMEM),
            pl.BlockSpec(memory_space=pl.ANY),
            pl.BlockSpec(memory_space=pltpu.VMEM),
        ],
        out_specs=pl.BlockSpec(memory_space=pltpu.VMEM),
        scratch_shapes=[
            pltpu.VMEM((out_len, nc * width), jnp.bfloat16),
            pltpu.VMEM((nc * width, k_all), jnp.bfloat16),
            pltpu.VMEM((nc, k_all, length), jnp.bfloat16),
            pltpu.SemaphoreType.DMA((nc,)),
        ],
        compiler_params=pltpu.CompilerParams(vmem_limit_bytes=48 * 1024 * 1024),
        cost_estimate=pl.CostEstimate(
            flops=2 * out_len * nc * width * k_all,
            bytes_accessed=templates2.size * 2 + out_len * (k_all + LANES) * 4,
            transcendentals=0,
        ),
    )(valid, waveform, templates2, mt)


def halving_steps(blocks, me, bits, axis, count, remaining):
    remaining = list(remaining)
    for bit in bits:
        pos = remaining.index(bit)
        mine = (me >> bit) & 1
        keep = lax.dynamic_index_in_dim(blocks, mine, axis=pos, keepdims=False)
        send = lax.dynamic_index_in_dim(blocks, 1 - mine, axis=pos, keepdims=False)
        perm = [(j, j ^ (1 << bit)) for j in range(count)]
        blocks = keep + lax.ppermute(send, axis, perm)
        remaining.pop(pos)
    return blocks


def halving_reduce_scatter(x, axis, split):
    count = lax.axis_size(axis)
    if count & (count - 1):
        natural = lax.psum_scatter(jnp.flip(x, 0), axis, scatter_dimension=0, tiled=True)
        return jnp.flip(natural, 0)
    me = count - 1 - lax.axis_index(axis)
    rows, cols = x.shape
    nbits = count.bit_length() - 1
    blocks = x.reshape((2,) * nbits + (rows // count, cols))
    every = list(range(nbits - 1, -1, -1))
    if nbits < 3:
        return halving_steps(blocks, me, list(range(nbits)), axis, count, every)
    blocks = halving_steps(blocks, me, [0], axis, count, every)
    rest = every[:-1]
    first = halving_steps(blocks[..., :split], me, list(range(1, nbits)), axis, count, rest)
    order = [2, 1] + list(range(3, nbits))
    second = halving_steps(blocks[..., split:], me, order, axis, count, rest)
    return jnp.concatenate([first, second], axis=-1)


def on_device(waveform, templates, moveouts, valid):
    k_all = templates.shape[0]
    templates2 = templates.reshape(k_all, -1)
    both = local_corr(valid, waveform, templates2, moveouts.T)
    summed = jnp.flip(halving_reduce_scatter(both, "chan", k_all // 2), axis=0)
    scale = jnp.sqrt(summed[:, k_all] + 1e-06)
    best = jnp.max(summed[:, :k_all] / scale[:, None], axis=1)
    return best


def solution(mesh):
    placed = (P("chan", "win"), P(None, "chan", None), P(None, "chan"), P("chan"))
    return jax.shard_map(
        on_device, mesh=mesh, in_specs=placed, out_specs=P(("win", "chan")), check_vma=False
    )
```

```python
import functools

import jax
import jax.numpy as jnp
from jax import lax
from jax.experimental import pallas as pl
from jax.experimental.pallas import tpu as pltpu
from jax.sharding import PartitionSpec as P

MAXSHIFT = 128
LANES = 128
PIECES = 4


def place_block(tr, mrow):
    rows, cols = tr.shape
    width = rows + MAXSHIFT
    fine = jnp.concatenate([tr, jnp.zeros((8, cols), tr.dtype)], axis=0)
    for level in range(3):
        amount = 1 << level
        moved = pltpu.roll(fine, amount, 0)
        fine = jnp.where((mrow >> level) & 1 == 1, moved, fine)
    x = jnp.concatenate([fine, jnp.zeros((width - fine.shape[0], cols), tr.dtype)], axis=0)
    for level in range(3, (MAXSHIFT - 1).bit_length()):
        amount = 1 << level
        moved = jnp.concatenate([jnp.zeros((amount, cols), x.dtype), x[: width - amount]], axis=0)
        x = jnp.where((mrow >> level) & 1 == 1, moved, x)
    return x


def build_hankel(valid_ref, w_ref, h_ref, out_ref, k_all, width):
    nc, span = w_ref.shape
    out_len = span - width
    q = jnp.zeros((1, span), jnp.float32)
    for c in range(nc):
        row = w_ref[pl.ds(c, 1), :].astype(jnp.float32)
        row = jnp.where(valid_ref[c] == 1, row, 0.0)
        q = q + row * row
        a = pltpu.roll(jnp.broadcast_to(row, (out_len, span)), 1, 1, stride=1, stride_axis=0)
        h_ref[:, c * width:(c + 1) * width] = a[:, span - width:].astype(jnp.bfloat16)
    aq = pltpu.roll(jnp.broadcast_to(q, (out_len, span)), 1, 1, stride=1, stride_axis=0)
    energy = jnp.sum(aq[:, span - width:], axis=1, keepdims=True)
    out_ref[:, k_all:] = jnp.broadcast_to(energy, (out_len, out_ref.shape[1] - k_all))


def place_and_multiply(k_start, k_all, t_hbm, m_ref, h_ref, out_ref, p_scr, t_buf, sems):
    nc = m_ref.shape[0]
    length = t_hbm.shape[1] // nc
    width = length + MAXSHIFT
    copies = []
    for c in range(nc):
        copy = pltpu.make_async_copy(
            t_hbm.at[pl.ds(k_start, k_all), pl.ds(c * length, length)], t_buf.at[c], sems.at[c]
        )
        copy.start()
        copies.append(copy)
    return copies, width


def multiply_rest(k_start, k_all, copies, width, m_ref, h_ref, out_ref, p_scr, t_buf):
    nc = m_ref.shape[0]
    length = t_buf.shape[2]
    ri = lax.broadcasted_iota(jnp.int32, (length, length), 0)
    ci = lax.broadcasted_iota(jnp.int32, (length, length), 1)
    eye = jnp.where(ri == ci, 1.0, 0.0).astype(jnp.bfloat16)
    for c in range(nc):
        copies[c].wait()

        def body(kc, carry):
            k0 = pl.multiple_of(kc * LANES, LANES)
            tk = t_buf[c, pl.ds(k0, LANES), :]
            tr = lax.dot_general(
                eye, tk, (((1,), (1,)), ((), ())), preferred_element_type=jnp.float32
            )
            mrow = m_ref[pl.ds(c, 1), pl.ds(k0 + k_start, LANES)]
            x = place_block(tr, mrow)
            p_scr[pl.ds(c * width, width), pl.ds(k0, LANES)] = x.astype(jnp.bfloat16)
            return carry

        lax.fori_loop(0, k_all // LANES, body, 0)
    step = min(256, k_all)
    for n0 in range(0, k_all, step):
        out_ref[:, n0:n0 + step] = jnp.dot(
            h_ref[...], p_scr[:, n0:n0 + step], preferred_element_type=jnp.float32
        )


def first_kernel(k_start, k_all, valid_ref, w_ref, t_hbm, m_ref, out_ref, h_ref,
                 p_scr, t_buf, sems):
    copies, width = place_and_multiply(
        k_start, k_all, t_hbm, m_ref, h_ref, out_ref, p_scr, t_buf, sems
    )
    build_hankel(valid_ref, w_ref, h_ref, out_ref, k_all, width)
    multiply_rest(k_start, k_all, copies, width, m_ref, h_ref, out_ref, p_scr, t_buf)


def later_kernel(k_start, k_all, h_ref, t_hbm, m_ref, out_ref, p_scr, t_buf, sems):
    copies, width = place_and_multiply(
        k_start, k_all, t_hbm, m_ref, h_ref, out_ref, p_scr, t_buf, sems
    )
    multiply_rest(k_start, k_all, copies, width, m_ref, h_ref, out_ref, p_scr, t_buf)


def local_corr(first, operands, k_start, k_all, nc, span):
    length = operands[-2].shape[1] // nc
    width = length + MAXSHIFT
    out_len = span - width
    scratch = [
        pltpu.VMEM((nc * width, k_all), jnp.bfloat16),
        pltpu.VMEM((nc, k_all, length), jnp.bfloat16),
        pltpu.SemaphoreType.DMA((nc,)),
    ]
    vmem = pl.BlockSpec(memory_space=pltpu.VMEM)
    cost = pl.CostEstimate(
        flops=2 * out_len * nc * width * k_all,
        bytes_accessed=k_all * nc * length * 2 + out_len * k_all * 4,
        transcendentals=0,
    )
    params = pltpu.CompilerParams(vmem_limit_bytes=48 * 1024 * 1024)
    if first:
        return pl.pallas_call(
            functools.partial(first_kernel, k_start, k_all),
            out_shape=(
                jax.ShapeDtypeStruct((out_len, k_all + LANES), jnp.float32),
                jax.ShapeDtypeStruct((out_len, nc * width), jnp.bfloat16),
            ),
            in_specs=[pl.BlockSpec(memory_space=pltpu.SMEM), vmem,
                      pl.BlockSpec(memory_space=pl.ANY), vmem],
            out_specs=(vmem, vmem),
            scratch_shapes=scratch,
            compiler_params=params,
            cost_estimate=cost,
        )(*operands)
    return pl.pallas_call(
        functools.partial(later_kernel, k_start, k_all),
        out_shape=jax.ShapeDtypeStruct((out_len, k_all), jnp.float32),
        in_specs=[vmem, pl.BlockSpec(memory_space=pl.ANY), vmem],
        out_specs=vmem,
        scratch_shapes=scratch,
        compiler_params=params,
        cost_estimate=cost,
    )(*operands)


def halving_steps(blocks, me, bits, axis, count, remaining):
    remaining = list(remaining)
    for bit in bits:
        pos = remaining.index(bit)
        mine = (me >> bit) & 1
        keep = lax.dynamic_index_in_dim(blocks, mine, axis=pos, keepdims=False)
        send = lax.dynamic_index_in_dim(blocks, 1 - mine, axis=pos, keepdims=False)
        perm = [(j, j ^ (1 << bit)) for j in range(count)]
        blocks = keep + lax.ppermute(send, axis, perm)
        remaining.pop(pos)
    return blocks


def halving_reduce_scatter(x, axis, swap):
    count = lax.axis_size(axis)
    if count & (count - 1):
        natural = lax.psum_scatter(jnp.flip(x, 0), axis, scatter_dimension=0, tiled=True)
        return jnp.flip(natural, 0)
    me = count - 1 - lax.axis_index(axis)
    rows, cols = x.shape
    nbits = count.bit_length() - 1
    blocks = x.reshape((2,) * nbits + (rows // count, cols))
    order = list(range(nbits))
    if swap and nbits >= 3:
        order[1], order[2] = order[2], order[1]
    return halving_steps(blocks, me, order, axis, count, list(range(nbits - 1, -1, -1)))


def on_device(waveform, templates, moveouts, valid):
    k_all = templates.shape[0]
    templates2 = templates.reshape(k_all, -1)
    nc, span = waveform.shape
    mt = moveouts.T
    pieces = PIECES if k_all % (PIECES * LANES) == 0 else 1
    size = k_all // pieces
    first, hankel = local_corr(True, (valid, waveform, templates2, mt), 0, size, nc, span)
    parts = [halving_reduce_scatter(first, "chan", False)]
    for piece in range(1, pieces):
        out = local_corr(False, (hankel, templates2, mt), piece * size, size, nc, span)
        parts.append(halving_reduce_scatter(out, "chan", piece % 2 == 1))
    summed = jnp.concatenate(parts[1:] + parts[:1], axis=-1)
    summed = jnp.flip(summed, axis=0)
    scale = jnp.sqrt(summed[:, k_all] + 1e-06)
    best = jnp.max(summed[:, :k_all] / scale[:, None], axis=1)
    return best


def solution(mesh):
    placed = (P("chan", "win"), P(None, "chan", None), P(None, "chan"), P("chan"))
    return jax.shard_map(
        on_device, mesh=mesh, in_specs=placed, out_specs=P(("win", "chan")), check_vma=False
    )
```

```python
import jax
import jax.numpy as jnp
from jax import lax
from jax.experimental import pallas as pl
from jax.experimental.pallas import tpu as pltpu
from jax.sharding import PartitionSpec as P

MAXSHIFT = 128
LANES = 128


def place_block(tr, mrow):
    rows, cols = tr.shape
    width = rows + MAXSHIFT
    fine = jnp.concatenate([tr, jnp.zeros((8, cols), tr.dtype)], axis=0)
    for level in range(3):
        amount = 1 << level
        moved = pltpu.roll(fine, amount, 0)
        fine = jnp.where((mrow >> level) & 1 == 1, moved, fine)
    x = jnp.concatenate([fine, jnp.zeros((width - fine.shape[0], cols), tr.dtype)], axis=0)
    for level in range(3, (MAXSHIFT - 1).bit_length()):
        amount = 1 << level
        moved = jnp.concatenate([jnp.zeros((amount, cols), x.dtype), x[: width - amount]], axis=0)
        x = jnp.where((mrow >> level) & 1 == 1, moved, x)
    return x


def corr_kernel(valid_ref, w_ref, t_hbm, m_ref, out_ref, h_scr, p_scr, t_buf, sems):
    nc, span = w_ref.shape
    k_all = t_hbm.shape[0]
    length = t_hbm.shape[1] // nc
    width = length + MAXSHIFT
    out_len = span - width
    copies = []
    for c in range(nc):
        copy = pltpu.make_async_copy(
            t_hbm.at[:, pl.ds(c * length, length)], t_buf.at[c], sems.at[c]
        )
        copy.start()
        copies.append(copy)
    q = jnp.zeros((1, span), jnp.float32)
    for c in range(nc):
        row = w_ref[pl.ds(c, 1), :].astype(jnp.float32)
        row = jnp.where(valid_ref[c] == 1, row, 0.0)
        q = q + row * row
        a = pltpu.roll(jnp.broadcast_to(row, (out_len, span)), 1, 1, stride=1, stride_axis=0)
        h_scr[:, c * width:(c + 1) * width] = a[:, span - width:].astype(jnp.bfloat16)
    aq = pltpu.roll(jnp.broadcast_to(q, (out_len, span)), 1, 1, stride=1, stride_axis=0)
    energy = jnp.sum(aq[:, span - width:], axis=1, keepdims=True)
    out_ref[:, k_all:] = jnp.broadcast_to(energy, (out_len, out_ref.shape[1] - k_all))

    ri = lax.broadcasted_iota(jnp.int32, (length, length), 0)
    ci = lax.broadcasted_iota(jnp.int32, (length, length), 1)
    eye = jnp.where(ri == ci, 1.0, 0.0).astype(jnp.bfloat16)
    for c in range(nc):
        copies[c].wait()

        def body(kc, carry):
            k0 = pl.multiple_of(kc * LANES, LANES)
            tk = t_buf[c, pl.ds(k0, LANES), :]
            tr = lax.dot_general(
                eye, tk, (((1,), (1,)), ((), ())), preferred_element_type=jnp.float32
            )
            mrow = m_ref[pl.ds(c, 1), pl.ds(k0, LANES)]
            x = place_block(tr, mrow)
            p_scr[pl.ds(c * width, width), pl.ds(k0, LANES)] = x.astype(jnp.bfloat16)
            return carry

        lax.fori_loop(0, k_all // LANES, body, 0)
    step = 256
    for n0 in range(0, k_all, step):
        out_ref[:, n0:n0 + step] = jnp.dot(
            h_scr[...], p_scr[:, n0:n0 + step], preferred_element_type=jnp.float32
        )


def local_corr(valid, waveform, templates2, mt):
    nc, span = waveform.shape
    k_all = templates2.shape[0]
    length = templates2.shape[1] // nc
    width = length + MAXSHIFT
    out_len = span - width
    return pl.pallas_call(
        corr_kernel,
        out_shape=jax.ShapeDtypeStruct((out_len, k_all + LANES), jnp.float32),
        in_specs=[
            pl.BlockSpec(memory_space=pltpu.SMEM),
            pl.BlockSpec(memory_space=pltpu.VMEM),
            pl.BlockSpec(memory_space=pl.ANY),
            pl.BlockSpec(memory_space=pltpu.VMEM),
        ],
        out_specs=pl.BlockSpec(memory_space=pltpu.VMEM),
        scratch_shapes=[
            pltpu.VMEM((out_len, nc * width), jnp.bfloat16),
            pltpu.VMEM((nc * width, k_all), jnp.bfloat16),
            pltpu.VMEM((nc, k_all, length), jnp.bfloat16),
            pltpu.SemaphoreType.DMA((nc,)),
        ],
        compiler_params=pltpu.CompilerParams(vmem_limit_bytes=48 * 1024 * 1024),
        cost_estimate=pl.CostEstimate(
            flops=2 * out_len * nc * width * k_all,
            bytes_accessed=templates2.size * 2 + out_len * (k_all + LANES) * 4,
            transcendentals=0,
        ),
    )(valid, waveform, templates2, mt)


def halving_steps(blocks, me, bits, axis, count, remaining):
    remaining = list(remaining)
    for bit in bits:
        pos = remaining.index(bit)
        mine = (me >> bit) & 1
        keep = lax.dynamic_index_in_dim(blocks, mine, axis=pos, keepdims=False)
        send = lax.dynamic_index_in_dim(blocks, 1 - mine, axis=pos, keepdims=False)
        perm = [(j, j ^ (1 << bit)) for j in range(count)]
        blocks = keep + lax.ppermute(send, axis, perm)
        remaining.pop(pos)
    return blocks


def halving_reduce_scatter(x, axis, split):
    count = lax.axis_size(axis)
    if count & (count - 1):
        natural = lax.psum_scatter(jnp.flip(x, 0), axis, scatter_dimension=0, tiled=True)
        return jnp.flip(natural, 0)
    me = count - 1 - lax.axis_index(axis)
    rows, cols = x.shape
    nbits = count.bit_length() - 1
    blocks = x.reshape((2,) * nbits + (rows // count, cols))
    every = list(range(nbits - 1, -1, -1))
    if nbits < 3:
        return halving_steps(blocks, me, list(range(nbits)), axis, count, every)
    blocks = halving_steps(blocks, me, [0], axis, count, every)
    rest = every[:-1]
    first = halving_steps(blocks[..., :split], me, [1, 2], axis, count, rest)
    second = halving_steps(blocks[..., split:], me, [2, 1], axis, count, rest)
    joined = jnp.concatenate([first, second], axis=-1)
    return halving_steps(joined, me, list(range(3, nbits)), axis, count, rest[:-2])


def on_device(waveform, templates, moveouts, valid):
    k_all = templates.shape[0]
    templates2 = templates.reshape(k_all, -1)
    both = local_corr(valid, waveform, templates2, moveouts.T)
    summed = jnp.flip(halving_reduce_scatter(both, "chan", k_all // 2), axis=0)
    scale = jnp.sqrt(summed[:, k_all] + 1e-06)
    best = jnp.max(summed[:, :k_all] / scale[:, None], axis=1)
    return best


def solution(mesh):
    placed = (P("chan", "win"), P(None, "chan", None), P(None, "chan"), P("chan"))
    return jax.shard_map(
        on_device, mesh=mesh, in_specs=placed, out_specs=P(("win", "chan")), check_vma=False
    )
```

```python
import jax
import jax.numpy as jnp
from jax import lax
from jax.experimental import pallas as pl
from jax.experimental.pallas import tpu as pltpu
from jax.sharding import PartitionSpec as P

MAXSHIFT = 128
LANES = 128


def place_block(tr, mrow):
    rows, cols = tr.shape
    x = jnp.concatenate([tr, jnp.zeros((8, cols), tr.dtype)], axis=0)
    for level in range(3):
        amount = 1 << level
        moved = pltpu.roll(x, amount, 0)
        x = jnp.where((mrow >> level) & 1 == 1, moved, x)
    for level in range(3, (MAXSHIFT - 1).bit_length()):
        if level == 4:
            x = x.astype(jnp.bfloat16)
        pad = jnp.zeros((1 << level, cols), x.dtype)
        x = jnp.where(
            (mrow >> level) & 1 == 1,
            jnp.concatenate([pad, x], axis=0),
            jnp.concatenate([x, pad], axis=0),
        )
    return x


def corr_kernel(valid_ref, w_ref, t_hbm, m_ref, out_ref, h_scr, p_scr, t_buf, sems):
    nc, span = w_ref.shape
    k_all = t_hbm.shape[0]
    length = t_hbm.shape[1] // nc
    width = length + MAXSHIFT
    out_len = span - width
    copies = []
    for c in range(nc):
        copy = pltpu.make_async_copy(
            t_hbm.at[:, pl.ds(c * length, length)], t_buf.at[c], sems.at[c]
        )
        copy.start()
        copies.append(copy)
    q = jnp.zeros((1, span), jnp.float32)
    for c in range(nc):
        row = w_ref[pl.ds(c, 1), :].astype(jnp.float32)
        row = jnp.where(valid_ref[c] == 1, row, 0.0)
        q = q + row * row
        a = pltpu.roll(jnp.broadcast_to(row, (out_len, span)), 1, 1, stride=1, stride_axis=0)
        h_scr[:, c * width:(c + 1) * width] = a[:, span - width:].astype(jnp.bfloat16)
    aq = pltpu.roll(jnp.broadcast_to(q, (out_len, span)), 1, 1, stride=1, stride_axis=0)
    energy = jnp.sum(aq[:, span - width:], axis=1, keepdims=True)
    out_ref[:, k_all:] = jnp.broadcast_to(energy, (out_len, out_ref.shape[1] - k_all))

    ri = lax.broadcasted_iota(jnp.int32, (length, length), 0)
    ci = lax.broadcasted_iota(jnp.int32, (length, length), 1)
    eye = jnp.where(ri == ci, 1.0, 0.0).astype(jnp.bfloat16)
    for c in range(nc):
        copies[c].wait()

        def body(kc, carry):
            k0 = pl.multiple_of(kc * LANES, LANES)
            tk = t_buf[c, pl.ds(k0, LANES), :]
            tr = lax.dot_general(
                eye, tk, (((1,), (1,)), ((), ())), preferred_element_type=jnp.float32
            )
            mrow = m_ref[pl.ds(c, 1), pl.ds(k0, LANES)]
            x = place_block(tr, mrow)
            p_scr[pl.ds(c * width, width), pl.ds(k0, LANES)] = x
            return carry

        lax.fori_loop(0, k_all // LANES, body, 0)
    step = 256
    for n0 in range(0, k_all, step):
        out_ref[:, n0:n0 + step] = jnp.dot(
            h_scr[...], p_scr[:, n0:n0 + step], preferred_element_type=jnp.float32
        )


def local_corr(valid, waveform, templates2, mt):
    nc, span = waveform.shape
    k_all = templates2.shape[0]
    length = templates2.shape[1] // nc
    width = length + MAXSHIFT
    out_len = span - width
    return pl.pallas_call(
        corr_kernel,
        out_shape=jax.ShapeDtypeStruct((out_len, k_all + LANES), jnp.float32),
        in_specs=[
            pl.BlockSpec(memory_space=pltpu.SMEM),
            pl.BlockSpec(memory_space=pltpu.VMEM),
            pl.BlockSpec(memory_space=pl.ANY),
            pl.BlockSpec(memory_space=pltpu.VMEM),
        ],
        out_specs=pl.BlockSpec(memory_space=pltpu.VMEM),
        scratch_shapes=[
            pltpu.VMEM((out_len, nc * width), jnp.bfloat16),
            pltpu.VMEM((nc * width, k_all), jnp.bfloat16),
            pltpu.VMEM((nc, k_all, length), jnp.bfloat16),
            pltpu.SemaphoreType.DMA((nc,)),
        ],
        compiler_params=pltpu.CompilerParams(vmem_limit_bytes=48 * 1024 * 1024),
        cost_estimate=pl.CostEstimate(
            flops=2 * out_len * nc * width * k_all,
            bytes_accessed=templates2.size * 2 + out_len * (k_all + LANES) * 4,
            transcendentals=0,
        ),
    )(valid, waveform, templates2, mt)


def halving_steps(blocks, me, bits, axis, count, remaining):
    remaining = list(remaining)
    for bit in bits:
        pos = remaining.index(bit)
        mine = (me >> bit) & 1
        keep = lax.dynamic_index_in_dim(blocks, mine, axis=pos, keepdims=False)
        send = lax.dynamic_index_in_dim(blocks, 1 - mine, axis=pos, keepdims=False)
        perm = [(j, j ^ (1 << bit)) for j in range(count)]
        blocks = keep + lax.ppermute(send, axis, perm)
        remaining.pop(pos)
    return blocks


def halving_reduce_scatter(x, axis, split):
    count = lax.axis_size(axis)
    if count & (count - 1):
        natural = lax.psum_scatter(jnp.flip(x, 0), axis, scatter_dimension=0, tiled=True)
        return jnp.flip(natural, 0)
    me = count - 1 - lax.axis_index(axis)
    rows, cols = x.shape
    nbits = count.bit_length() - 1
    blocks = x.reshape((2,) * nbits + (rows // count, cols))
    every = list(range(nbits - 1, -1, -1))
    if nbits < 3:
        return halving_steps(blocks, me, list(range(nbits)), axis, count, every)
    blocks = halving_steps(blocks, me, [0], axis, count, every)
    rest = every[:-1]
    first = halving_steps(blocks[..., :split], me, [1, 2], axis, count, rest)
    second = halving_steps(blocks[..., split:], me, [2, 1], axis, count, rest)
    joined = jnp.concatenate([first, second], axis=-1)
    return halving_steps(joined, me, list(range(3, nbits)), axis, count, rest[:-2])


def on_device(waveform, templates, moveouts, valid):
    k_all = templates.shape[0]
    templates2 = templates.reshape(k_all, -1)
    both = local_corr(valid, waveform, templates2, moveouts.T)
    summed = jnp.flip(halving_reduce_scatter(both, "chan", k_all // 2), axis=0)
    scale = jnp.sqrt(summed[:, k_all] + 1e-06)
    best = jnp.max(summed[:, :k_all] / scale[:, None], axis=1)
    return best


def solution(mesh):
    placed = (P("chan", "win"), P(None, "chan", None), P(None, "chan"), P("chan"))
    return jax.shard_map(
        on_device, mesh=mesh, in_specs=placed, out_specs=P(("win", "chan")), check_vma=False
    )
```

```python
import jax
import jax.numpy as jnp
from jax import lax
from jax.experimental import pallas as pl
from jax.experimental.pallas import tpu as pltpu
from jax.sharding import PartitionSpec as P

MAXSHIFT = 128
LANES = 128


def place_block(tr, mrow):
    rows, cols = tr.shape
    x = jnp.concatenate([tr, jnp.zeros((8, cols), tr.dtype)], axis=0)
    for level in range(3):
        amount = 1 << level
        moved = pltpu.roll(x, amount, 0)
        x = jnp.where((mrow >> level) & 1 == 1, moved, x)
    for level in range(3, (MAXSHIFT - 1).bit_length()):
        if level == 4:
            x = x.astype(jnp.bfloat16)
        pad = jnp.zeros((1 << level, cols), x.dtype)
        x = jnp.where(
            (mrow >> level) & 1 == 1,
            jnp.concatenate([pad, x], axis=0),
            jnp.concatenate([x, pad], axis=0),
        )
    return x


def corr_kernel(valid_ref, w_ref, t_hbm, m_ref, out_ref, h_scr, p_scr, t_buf, tr_scr, sems):
    nc, span = w_ref.shape
    k_all = t_hbm.shape[0]
    length = t_hbm.shape[1] // nc
    width = length + MAXSHIFT
    out_len = span - width
    copies = []
    for c in range(nc):
        copy = pltpu.make_async_copy(
            t_hbm.at[:, pl.ds(c * length, length)], t_buf.at[c], sems.at[c]
        )
        copy.start()
        copies.append(copy)
    q = jnp.zeros((1, span), jnp.float32)
    for c in range(nc):
        row = w_ref[pl.ds(c, 1), :].astype(jnp.float32)
        row = jnp.where(valid_ref[c] == 1, row, 0.0)
        q = q + row * row
        a = pltpu.roll(jnp.broadcast_to(row, (out_len, span)), 1, 1, stride=1, stride_axis=0)
        h_scr[:, c * width:(c + 1) * width] = a[:, span - width:].astype(jnp.bfloat16)
    aq = pltpu.roll(jnp.broadcast_to(q, (out_len, span)), 1, 1, stride=1, stride_axis=0)
    energy = jnp.sum(aq[:, span - width:], axis=1, keepdims=True)
    out_ref[:, k_all:] = jnp.broadcast_to(energy, (out_len, out_ref.shape[1] - k_all))

    ri = lax.broadcasted_iota(jnp.int32, (length, length), 0)
    ci = lax.broadcasted_iota(jnp.int32, (length, length), 1)
    eye = jnp.where(ri == ci, 1.0, 0.0).astype(jnp.bfloat16)
    for c in range(nc):
        copies[c].wait()
        tr_scr[...] = lax.dot_general(
            eye, t_buf[c], (((1,), (1,)), ((), ())), preferred_element_type=jnp.float32
        )

        def body(kc, carry):
            k0 = pl.multiple_of(kc * LANES, LANES)
            tr = tr_scr[:, pl.ds(k0, LANES)]
            mrow = m_ref[pl.ds(c, 1), pl.ds(k0, LANES)]
            x = place_block(tr, mrow)
            p_scr[pl.ds(c * width, width), pl.ds(k0, LANES)] = x
            return carry

        lax.fori_loop(0, k_all // LANES, body, 0)
    step = 256
    for n0 in range(0, k_all, step):
        out_ref[:, n0:n0 + step] = jnp.dot(
            h_scr[...], p_scr[:, n0:n0 + step], preferred_element_type=jnp.float32
        )


def local_corr(valid, waveform, templates2, mt):
    nc, span = waveform.shape
    k_all = templates2.shape[0]
    length = templates2.shape[1] // nc
    width = length + MAXSHIFT
    out_len = span - width
    return pl.pallas_call(
        corr_kernel,
        out_shape=jax.ShapeDtypeStruct((out_len, k_all + LANES), jnp.float32),
        in_specs=[
            pl.BlockSpec(memory_space=pltpu.SMEM),
            pl.BlockSpec(memory_space=pltpu.VMEM),
            pl.BlockSpec(memory_space=pl.ANY),
            pl.BlockSpec(memory_space=pltpu.VMEM),
        ],
        out_specs=pl.BlockSpec(memory_space=pltpu.VMEM),
        scratch_shapes=[
            pltpu.VMEM((out_len, nc * width), jnp.bfloat16),
            pltpu.VMEM((nc * width, k_all), jnp.bfloat16),
            pltpu.VMEM((nc, k_all, length), jnp.bfloat16),
            pltpu.VMEM((length, k_all), jnp.float32),
            pltpu.SemaphoreType.DMA((nc,)),
        ],
        compiler_params=pltpu.CompilerParams(vmem_limit_bytes=48 * 1024 * 1024),
        cost_estimate=pl.CostEstimate(
            flops=2 * out_len * nc * width * k_all,
            bytes_accessed=templates2.size * 2 + out_len * (k_all + LANES) * 4,
            transcendentals=0,
        ),
    )(valid, waveform, templates2, mt)


def halving_steps(blocks, me, bits, axis, count, remaining):
    remaining = list(remaining)
    for bit in bits:
        pos = remaining.index(bit)
        mine = (me >> bit) & 1
        keep = lax.dynamic_index_in_dim(blocks, mine, axis=pos, keepdims=False)
        send = lax.dynamic_index_in_dim(blocks, 1 - mine, axis=pos, keepdims=False)
        perm = [(j, j ^ (1 << bit)) for j in range(count)]
        blocks = keep + lax.ppermute(send, axis, perm)
        remaining.pop(pos)
    return blocks


def halving_reduce_scatter(x, axis, split):
    count = lax.axis_size(axis)
    if count & (count - 1):
        natural = lax.psum_scatter(jnp.flip(x, 0), axis, scatter_dimension=0, tiled=True)
        return jnp.flip(natural, 0)
    me = count - 1 - lax.axis_index(axis)
    rows, cols = x.shape
    nbits = count.bit_length() - 1
    blocks = x.reshape((2,) * nbits + (rows // count, cols))
    every = list(range(nbits - 1, -1, -1))
    if nbits < 3:
        return halving_steps(blocks, me, list(range(nbits)), axis, count, every)
    blocks = halving_steps(blocks, me, [0], axis, count, every)
    rest = every[:-1]
    first = halving_steps(blocks[..., :split], me, [1, 2], axis, count, rest)
    second = halving_steps(blocks[..., split:], me, [2, 1], axis, count, rest)
    joined = jnp.concatenate([first, second], axis=-1)
    return halving_steps(joined, me, list(range(3, nbits)), axis, count, rest[:-2])


def on_device(waveform, templates, moveouts, valid):
    k_all = templates.shape[0]
    templates2 = templates.reshape(k_all, -1)
    both = local_corr(valid, waveform, templates2, moveouts.T)
    summed = jnp.flip(halving_reduce_scatter(both, "chan", k_all // 2), axis=0)
    scale = jnp.sqrt(summed[:, k_all] + 1e-06)
    best = jnp.max(summed[:, :k_all] / scale[:, None], axis=1)
    return best


def solution(mesh):
    placed = (P("chan", "win"), P(None, "chan", None), P(None, "chan"), P("chan"))
    return jax.shard_map(
        on_device, mesh=mesh, in_specs=placed, out_specs=P(("win", "chan")), check_vma=False
    )
```

```python
import functools

import jax
import jax.numpy as jnp
from jax import lax
from jax.experimental import pallas as pl
from jax.experimental.pallas import tpu as pltpu
from jax.sharding import PartitionSpec as P

MAXSHIFT = 128
LANES = 128


def place_block(tr, mrow):
    rows, cols = tr.shape
    x = jnp.concatenate([tr, jnp.zeros((8, cols), tr.dtype)], axis=0)
    for level in range(3):
        amount = 1 << level
        moved = pltpu.roll(x, amount, 0)
        x = jnp.where((mrow >> level) & 1 == 1, moved, x)
    for level in range(3, (MAXSHIFT - 1).bit_length()):
        if level == 4:
            x = x.astype(jnp.bfloat16)
        pad = jnp.zeros((1 << level, cols), x.dtype)
        x = jnp.where(
            (mrow >> level) & 1 == 1,
            jnp.concatenate([pad, x], axis=0),
            jnp.concatenate([x, pad], axis=0),
        )
    return x


def corr_kernel(count, valid_ref, w_ref, t_hbm, m_ref, out_ref, h_scr, p_scr, t_buf, tr_scr, sems):
    nc, span = w_ref.shape
    k_all = t_hbm.shape[0]
    length = t_hbm.shape[1] // nc
    width = length + MAXSHIFT
    out_len = span - width
    copies = []
    for c in range(nc):
        copy = pltpu.make_async_copy(
            t_hbm.at[:, pl.ds(c * length, length)], t_buf.at[c], sems.at[c]
        )
        copy.start()
        copies.append(copy)
    q = jnp.zeros((1, span), jnp.float32)
    for c in range(nc):
        row = w_ref[pl.ds(c, 1), :].astype(jnp.float32)
        row = jnp.where(valid_ref[c] == 1, row, 0.0)
        q = q + row * row
        a = pltpu.roll(jnp.broadcast_to(row, (out_len, span)), 1, 1, stride=1, stride_axis=0)
        h_scr[:, c * width:(c + 1) * width] = a[:, span - width:].astype(jnp.bfloat16)
    aq = pltpu.roll(jnp.broadcast_to(q, (out_len, span)), 1, 1, stride=1, stride_axis=0)
    energy = jnp.sum(aq[:, span - width:], axis=1, keepdims=True)
    rows = out_len // count
    brows = out_ref.shape[0] // count
    corr_rows = (k_all // LANES) * rows
    energy_row = jnp.transpose(jnp.broadcast_to(energy, (out_len, LANES)))[0:1, :]
    tail = [energy_row[:, i:i + LANES] for i in range(0, out_len, LANES)]
    tail.append(jnp.zeros((brows - corr_rows - len(tail), LANES), jnp.float32))
    tail = jnp.concatenate(tail, axis=0)
    for b in range(count):
        out_ref[b * brows + corr_rows:(b + 1) * brows, :] = tail

    ri = lax.broadcasted_iota(jnp.int32, (length, length), 0)
    ci = lax.broadcasted_iota(jnp.int32, (length, length), 1)
    eye = jnp.where(ri == ci, 1.0, 0.0).astype(jnp.bfloat16)
    for c in range(nc):
        copies[c].wait()
        tr_scr[...] = lax.dot_general(
            eye, t_buf[c], (((1,), (1,)), ((), ())), preferred_element_type=jnp.float32
        )

        def body(kc, carry):
            k0 = pl.multiple_of(kc * LANES, LANES)
            tr = tr_scr[:, pl.ds(k0, LANES)]
            mrow = m_ref[pl.ds(c, 1), pl.ds(k0, LANES)]
            x = place_block(tr, mrow)
            p_scr[pl.ds(c * width, width), pl.ds(k0, LANES)] = x
            return carry

        lax.fori_loop(0, k_all // LANES, body, 0)
    step = 256
    for n0 in range(0, k_all, step):
        res = jnp.dot(h_scr[...], p_scr[:, n0:n0 + step], preferred_element_type=jnp.float32)
        for sub in range(step // LANES):
            kt = n0 // LANES + sub
            for b in range(count):
                out_ref[b * brows + kt * rows:b * brows + (kt + 1) * rows, :] = res[
                    b * rows:(b + 1) * rows, sub * LANES:(sub + 1) * LANES
                ]


def local_corr(valid, waveform, templates2, mt, count):
    nc, span = waveform.shape
    k_all = templates2.shape[0]
    length = templates2.shape[1] // nc
    width = length + MAXSHIFT
    out_len = span - width
    brows = (k_all // LANES) * (out_len // count) + 8
    return pl.pallas_call(
        functools.partial(corr_kernel, count),
        out_shape=jax.ShapeDtypeStruct((count * brows, LANES), jnp.float32),
        in_specs=[
            pl.BlockSpec(memory_space=pltpu.SMEM),
            pl.BlockSpec(memory_space=pltpu.VMEM),
            pl.BlockSpec(memory_space=pl.ANY),
            pl.BlockSpec(memory_space=pltpu.VMEM),
        ],
        out_specs=pl.BlockSpec(memory_space=pltpu.VMEM),
        scratch_shapes=[
            pltpu.VMEM((out_len, nc * width), jnp.bfloat16),
            pltpu.VMEM((nc * width, k_all), jnp.bfloat16),
            pltpu.VMEM((nc, k_all, length), jnp.bfloat16),
            pltpu.VMEM((length, k_all), jnp.float32),
            pltpu.SemaphoreType.DMA((nc,)),
        ],
        compiler_params=pltpu.CompilerParams(vmem_limit_bytes=48 * 1024 * 1024),
        cost_estimate=pl.CostEstimate(
            flops=2 * out_len * nc * width * k_all,
            bytes_accessed=templates2.size * 2 + out_len * (k_all + LANES) * 4,
            transcendentals=0,
        ),
    )(valid, waveform, templates2, mt)


def halving_steps(blocks, me, bits, axis, count, remaining):
    remaining = list(remaining)
    for bit in bits:
        pos = remaining.index(bit)
        mine = (me >> bit) & 1
        keep = lax.dynamic_index_in_dim(blocks, mine, axis=pos, keepdims=False)
        send = lax.dynamic_index_in_dim(blocks, 1 - mine, axis=pos, keepdims=False)
        perm = [(j, j ^ (1 << bit)) for j in range(count)]
        blocks = keep + lax.ppermute(send, axis, perm)
        remaining.pop(pos)
    return blocks


def halving_reduce_scatter(x, axis, split):
    count = lax.axis_size(axis)
    brows = x.shape[0] // count
    if count & (count - 1):
        flipped = jnp.flip(x.reshape(count, brows, LANES), 0).reshape(x.shape)
        return lax.psum_scatter(flipped, axis, scatter_dimension=0, tiled=True)
    me = count - 1 - lax.axis_index(axis)
    nbits = count.bit_length() - 1
    blocks = x.reshape((2,) * nbits + (brows, LANES))
    every = list(range(nbits - 1, -1, -1))
    if nbits < 3:
        return halving_steps(blocks, me, list(range(nbits)), axis, count, every)
    blocks = halving_steps(blocks, me, [0], axis, count, every)
    rest = every[:-1]
    first = halving_steps(blocks[..., :split, :], me, [1, 2], axis, count, rest)
    second = halving_steps(blocks[..., split:, :], me, [2, 1], axis, count, rest)
    joined = jnp.concatenate([first, second], axis=-2)
    return halving_steps(joined, me, list(range(3, nbits)), axis, count, rest[:-2])


def on_device(waveform, templates, moveouts, valid):
    k_all = templates.shape[0]
    count = lax.axis_size("chan")
    out_len = waveform.shape[1] - templates.shape[2] - MAXSHIFT
    rows = out_len // count
    tiles = k_all // LANES
    templates2 = templates.reshape(k_all, -1)
    both = local_corr(valid, waveform, templates2, moveouts.T, count)
    mine = halving_reduce_scatter(both, "chan", (tiles // 2) * rows)
    corr = mine[: tiles * rows].reshape(tiles, rows, LANES)
    energy_all = mine[tiles * rows:tiles * rows + out_len // LANES].reshape(out_len)
    block = count - 1 - lax.axis_index("chan")
    energy = lax.dynamic_slice_in_dim(energy_all, block * rows, rows)
    scale = jnp.sqrt(energy + 1e-06)
    best = jnp.max(corr / scale[None, :, None], axis=(0, 2))
    return jnp.flip(best, axis=0)


def solution(mesh):
    placed = (P("chan", "win"), P(None, "chan", None), P(None, "chan"), P("chan"))
    return jax.shard_map(
        on_device, mesh=mesh, in_specs=placed, out_specs=P(("win", "chan")), check_vma=False
    )
```

```python
import functools

import jax
import jax.numpy as jnp
from jax import lax
from jax.experimental import pallas as pl
from jax.experimental.pallas import tpu as pltpu
from jax.sharding import PartitionSpec as P

MAXSHIFT = 128
LANES = 128


def place_block(tr, mrow):
    rows, cols = tr.shape
    x = jnp.concatenate([jnp.zeros((8, cols), tr.dtype), tr], axis=0)
    for level in range(3):
        amount = 1 << level
        moved = pltpu.roll(x, x.shape[0] - amount, 0)
        x = jnp.where((mrow >> level) & 1 == 1, moved, x)
    for level in range(3, (MAXSHIFT - 1).bit_length()):
        if level == 4:
            x = x.astype(jnp.bfloat16)
        pad = jnp.zeros((1 << level, cols), x.dtype)
        x = jnp.where(
            (mrow >> level) & 1 == 1,
            jnp.concatenate([x, pad], axis=0),
            jnp.concatenate([pad, x], axis=0),
        )
    return x


def corr_kernel(count, valid_ref, w_ref, t_hbm, m_ref, out_ref, h_scr, p_scr, t_buf, tr_scr, sems):
    nc, span = w_ref.shape
    k_all = t_hbm.shape[0]
    length = t_hbm.shape[1] // nc
    width = length + MAXSHIFT
    out_len = span - width
    copies = []
    for c in range(nc):
        copy = pltpu.make_async_copy(
            t_hbm.at[:, pl.ds(c * length, length)], t_buf.at[c], sems.at[c]
        )
        copy.start()
        copies.append(copy)
    rows_all = []
    for c in range(nc):
        row = w_ref[pl.ds(c, 1), :].astype(jnp.float32)
        rows_all.append(jnp.where(valid_ref[c] == 1, row, 0.0))
    ui = lax.broadcasted_iota(jnp.int32, (span, span), 0)
    vi = lax.broadcasted_iota(jnp.int32, (span, span), 1)
    flip_t = jnp.where(ui + vi == span - 1, 1.0, 0.0).astype(jnp.bfloat16)
    masked = jnp.concatenate(rows_all, axis=0).astype(jnp.bfloat16)
    wrev = jnp.dot(masked, flip_t, preferred_element_type=jnp.float32)
    q = jnp.sum(wrev * wrev, axis=0, keepdims=True)
    for c in range(nc):
        a = pltpu.roll(
            jnp.broadcast_to(wrev[c:c + 1, :], (out_len, span)), 0, 1, stride=1, stride_axis=0
        )
        h_scr[:, c * width:(c + 1) * width] = a[:, span - width:].astype(jnp.bfloat16)
    aq = pltpu.roll(jnp.broadcast_to(q, (out_len, span)), 0, 1, stride=1, stride_axis=0)
    energy = jnp.sum(aq[:, span - width:], axis=1, keepdims=True)
    rows = out_len // count
    brows = out_ref.shape[0] // count
    corr_rows = (k_all // LANES) * rows
    energy_row = jnp.transpose(jnp.broadcast_to(energy, (out_len, LANES)))[0:1, :]
    tail = [energy_row[:, i:i + LANES] for i in range(0, out_len, LANES)]
    tail.append(jnp.zeros((brows - corr_rows - len(tail), LANES), jnp.float32))
    tail = jnp.concatenate(tail, axis=0)
    for b in range(count):
        out_ref[b * brows + corr_rows:(b + 1) * brows, :] = tail

    ri = lax.broadcasted_iota(jnp.int32, (length, length), 0)
    ci = lax.broadcasted_iota(jnp.int32, (length, length), 1)
    eye = jnp.where(ri + ci == length - 1, 1.0, 0.0).astype(jnp.bfloat16)
    for c in range(nc):
        copies[c].wait()
        tr_scr[...] = lax.dot_general(
            eye, t_buf[c], (((1,), (1,)), ((), ())), preferred_element_type=jnp.float32
        )

        def body(kc, carry):
            k0 = pl.multiple_of(kc * LANES, LANES)
            tr = tr_scr[:, pl.ds(k0, LANES)]
            mrow = m_ref[pl.ds(c, 1), pl.ds(k0, LANES)]
            x = place_block(tr, mrow)
            p_scr[pl.ds(c * width, width), pl.ds(k0, LANES)] = x
            return carry

        lax.fori_loop(0, k_all // LANES, body, 0)
    step = 256
    for n0 in range(0, k_all, step):
        res = jnp.dot(h_scr[...], p_scr[:, n0:n0 + step], preferred_element_type=jnp.float32)
        for sub in range(step // LANES):
            kt = n0 // LANES + sub
            for b in range(count):
                out_ref[b * brows + kt * rows:b * brows + (kt + 1) * rows, :] = res[
                    b * rows:(b + 1) * rows, sub * LANES:(sub + 1) * LANES
                ]


def local_corr(valid, waveform, templates2, mt, count):
    nc, span = waveform.shape
    k_all = templates2.shape[0]
    length = templates2.shape[1] // nc
    width = length + MAXSHIFT
    out_len = span - width
    brows = (k_all // LANES) * (out_len // count) + 8
    return pl.pallas_call(
        functools.partial(corr_kernel, count),
        out_shape=jax.ShapeDtypeStruct((count * brows, LANES), jnp.float32),
        in_specs=[
            pl.BlockSpec(memory_space=pltpu.SMEM),
            pl.BlockSpec(memory_space=pltpu.VMEM),
            pl.BlockSpec(memory_space=pl.ANY),
            pl.BlockSpec(memory_space=pltpu.VMEM),
        ],
        out_specs=pl.BlockSpec(memory_space=pltpu.VMEM),
        scratch_shapes=[
            pltpu.VMEM((out_len, nc * width), jnp.bfloat16),
            pltpu.VMEM((nc * width, k_all), jnp.bfloat16),
            pltpu.VMEM((nc, k_all, length), jnp.bfloat16),
            pltpu.VMEM((length, k_all), jnp.float32),
            pltpu.SemaphoreType.DMA((nc,)),
        ],
        compiler_params=pltpu.CompilerParams(vmem_limit_bytes=48 * 1024 * 1024),
        cost_estimate=pl.CostEstimate(
            flops=2 * out_len * nc * width * k_all,
            bytes_accessed=templates2.size * 2 + out_len * (k_all + LANES) * 4,
            transcendentals=0,
        ),
    )(valid, waveform, templates2, mt)


def halving_steps(blocks, me, bits, axis, count, remaining):
    remaining = list(remaining)
    for bit in bits:
        pos = remaining.index(bit)
        mine = (me >> bit) & 1
        keep = lax.dynamic_index_in_dim(blocks, mine, axis=pos, keepdims=False)
        send = lax.dynamic_index_in_dim(blocks, 1 - mine, axis=pos, keepdims=False)
        perm = [(j, j ^ (1 << bit)) for j in range(count)]
        blocks = keep + lax.ppermute(send, axis, perm)
        remaining.pop(pos)
    return blocks


def halving_reduce_scatter(x, axis, split):
    count = lax.axis_size(axis)
    brows = x.shape[0] // count
    if count & (count - 1):
        return lax.psum_scatter(x, axis, scatter_dimension=0, tiled=True)
    me = lax.axis_index(axis)
    nbits = count.bit_length() - 1
    blocks = x.reshape((2,) * nbits + (brows, LANES))
    every = list(range(nbits - 1, -1, -1))
    if nbits < 3:
        return halving_steps(blocks, me, list(range(nbits)), axis, count, every)
    blocks = halving_steps(blocks, me, [0], axis, count, every)
    rest = every[:-1]
    first = halving_steps(blocks[..., :split, :], me, [1, 2], axis, count, rest)
    second = halving_steps(blocks[..., split:, :], me, [2, 1], axis, count, rest)
    joined = jnp.concatenate([first, second], axis=-2)
    return halving_steps(joined, me, list(range(3, nbits)), axis, count, rest[:-2])


def on_device(waveform, templates, moveouts, valid):
    k_all = templates.shape[0]
    count = lax.axis_size("chan")
    out_len = waveform.shape[1] - templates.shape[2] - MAXSHIFT
    rows = out_len // count
    tiles = k_all // LANES
    templates2 = templates.reshape(k_all, -1)
    both = local_corr(valid, waveform, templates2, moveouts.T, count)
    mine = halving_reduce_scatter(both, "chan", (tiles // 2) * rows)
    corr = mine[: tiles * rows].reshape(tiles, rows, LANES)
    energy_all = mine[tiles * rows:tiles * rows + out_len // LANES].reshape(out_len)
    energy = lax.dynamic_slice_in_dim(energy_all, lax.axis_index("chan") * rows, rows)
    scale = jnp.sqrt(energy + 1e-06)
    best = jnp.max(corr / scale[None, :, None], axis=(0, 2))
    return best


def solution(mesh):
    placed = (P("chan", "win"), P(None, "chan", None), P(None, "chan"), P("chan"))
    return jax.shard_map(
        on_device, mesh=mesh, in_specs=placed, out_specs=P(("win", "chan")), check_vma=False
    )
```

```python
import functools

import jax
import jax.numpy as jnp
from jax import lax
from jax.experimental import pallas as pl
from jax.experimental.pallas import tpu as pltpu
from jax.sharding import PartitionSpec as P

MAXSHIFT = 128
LANES = 128


def place_block(tr, mrow):
    rows, cols = tr.shape
    x = jnp.concatenate([tr, jnp.zeros((8, cols), tr.dtype)], axis=0)
    for level in range(3):
        amount = 1 << level
        moved = pltpu.roll(x, amount, 0)
        x = jnp.where((mrow >> level) & 1 == 1, moved, x)
    for level in range(3, (MAXSHIFT - 1).bit_length()):
        if level == 4:
            x = x.astype(jnp.bfloat16)
        pad = jnp.zeros((1 << level, cols), x.dtype)
        x = jnp.where(
            (mrow >> level) & 1 == 1,
            jnp.concatenate([pad, x], axis=0),
            jnp.concatenate([x, pad], axis=0),
        )
    return x


def corr_kernel(count, valid_ref, w_ref, t_hbm, m_ref, out_ref, h_scr, p_scr, t_buf, tr_scr, sems):
    nc, span = w_ref.shape
    k_all = t_hbm.shape[1]
    length = t_hbm.shape[2]
    width = length + MAXSHIFT
    out_len = span - width
    copies = []
    for c in range(nc):
        copy = pltpu.make_async_copy(
            t_hbm.at[c], t_buf.at[c], sems.at[c]
        )
        copy.start()
        copies.append(copy)
    q = jnp.zeros((1, span), jnp.float32)
    for c in range(nc):
        row = w_ref[pl.ds(c, 1), :].astype(jnp.float32)
        row = jnp.where(valid_ref[c] == 1, row, 0.0)
        q = q + row * row
        a = pltpu.roll(jnp.broadcast_to(row, (out_len, span)), 1, 1, stride=1, stride_axis=0)
        h_scr[:, c * width:(c + 1) * width] = a[:, span - width:].astype(jnp.bfloat16)
    aq = pltpu.roll(jnp.broadcast_to(q, (out_len, span)), 1, 1, stride=1, stride_axis=0)
    energy = jnp.sum(aq[:, span - width:], axis=1, keepdims=True)
    rows = out_len // count
    brows = out_ref.shape[0] // count
    corr_rows = (k_all // LANES) * rows
    energy_row = jnp.transpose(jnp.broadcast_to(energy, (out_len, LANES)))[0:1, :]
    tail = [energy_row[:, i:i + LANES] for i in range(0, out_len, LANES)]
    tail.append(jnp.zeros((brows - corr_rows - len(tail), LANES), jnp.float32))
    tail = jnp.concatenate(tail, axis=0)
    for b in range(count):
        out_ref[b * brows + corr_rows:(b + 1) * brows, :] = tail

    ri = lax.broadcasted_iota(jnp.int32, (length, length), 0)
    ci = lax.broadcasted_iota(jnp.int32, (length, length), 1)
    eye = jnp.where(ri == ci, 1.0, 0.0).astype(jnp.bfloat16)
    for c in range(nc):
        copies[c].wait()
        tr_scr[...] = lax.dot_general(
            eye, t_buf[c], (((1,), (1,)), ((), ())), preferred_element_type=jnp.float32
        )

        def body(kc, carry):
            k0 = pl.multiple_of(kc * LANES, LANES)
            tr = tr_scr[:, pl.ds(k0, LANES)]
            mrow = m_ref[pl.ds(c, 1), pl.ds(k0, LANES)]
            x = place_block(tr, mrow)
            p_scr[pl.ds(c * width, width), pl.ds(k0, LANES)] = x
            return carry

        lax.fori_loop(0, k_all // LANES, body, 0)
    step = 256
    for n0 in range(0, k_all, step):
        res = jnp.dot(h_scr[...], p_scr[:, n0:n0 + step], preferred_element_type=jnp.float32)
        for sub in range(step // LANES):
            kt = n0 // LANES + sub
            for b in range(count):
                out_ref[b * brows + kt * rows:b * brows + (kt + 1) * rows, :] = res[
                    b * rows:(b + 1) * rows, sub * LANES:(sub + 1) * LANES
                ]


def local_corr(valid, waveform, templates2, mt, count):
    nc, span = waveform.shape
    k_all = templates2.shape[1]
    length = templates2.shape[2]
    width = length + MAXSHIFT
    out_len = span - width
    brows = (k_all // LANES) * (out_len // count) + 8
    return pl.pallas_call(
        functools.partial(corr_kernel, count),
        out_shape=jax.ShapeDtypeStruct((count * brows, LANES), jnp.float32),
        in_specs=[
            pl.BlockSpec(memory_space=pltpu.SMEM),
            pl.BlockSpec(memory_space=pltpu.VMEM),
            pl.BlockSpec(memory_space=pl.ANY),
            pl.BlockSpec(memory_space=pltpu.VMEM),
        ],
        out_specs=pl.BlockSpec(memory_space=pltpu.VMEM),
        scratch_shapes=[
            pltpu.VMEM((out_len, nc * width), jnp.bfloat16),
            pltpu.VMEM((nc * width, k_all), jnp.bfloat16),
            pltpu.VMEM((nc, k_all, length), jnp.bfloat16),
            pltpu.VMEM((length, k_all), jnp.float32),
            pltpu.SemaphoreType.DMA((nc,)),
        ],
        compiler_params=pltpu.CompilerParams(vmem_limit_bytes=48 * 1024 * 1024),
        cost_estimate=pl.CostEstimate(
            flops=2 * out_len * nc * width * k_all,
            bytes_accessed=templates2.size * 2 + out_len * (k_all + LANES) * 4,
            transcendentals=0,
        ),
    )(valid, waveform, templates2, mt)


def halving_steps(blocks, me, bits, axis, count, remaining):
    remaining = list(remaining)
    for bit in bits:
        pos = remaining.index(bit)
        mine = (me >> bit) & 1
        keep = lax.dynamic_index_in_dim(blocks, mine, axis=pos, keepdims=False)
        send = lax.dynamic_index_in_dim(blocks, 1 - mine, axis=pos, keepdims=False)
        perm = [(j, j ^ (1 << bit)) for j in range(count)]
        blocks = keep + lax.ppermute(send, axis, perm)
        remaining.pop(pos)
    return blocks


def halving_reduce_scatter(x, axis, split):
    count = lax.axis_size(axis)
    brows = x.shape[0] // count
    if count & (count - 1):
        flipped = jnp.flip(x.reshape(count, brows, LANES), 0).reshape(x.shape)
        return lax.psum_scatter(flipped, axis, scatter_dimension=0, tiled=True)
    me = count - 1 - lax.axis_index(axis)
    nbits = count.bit_length() - 1
    blocks = x.reshape((2,) * nbits + (brows, LANES))
    every = list(range(nbits - 1, -1, -1))
    if nbits < 3:
        return halving_steps(blocks, me, list(range(nbits)), axis, count, every)
    blocks = halving_steps(blocks, me, [0], axis, count, every)
    rest = every[:-1]
    first = halving_steps(blocks[..., :split, :], me, [1, 2], axis, count, rest)
    second = halving_steps(blocks[..., split:, :], me, [2, 1], axis, count, rest)
    joined = jnp.concatenate([first, second], axis=-2)
    return halving_steps(joined, me, list(range(3, nbits)), axis, count, rest[:-2])


def on_device(waveform, templates, moveouts, valid):
    k_all = templates.shape[0]
    count = lax.axis_size("chan")
    out_len = waveform.shape[1] - templates.shape[2] - MAXSHIFT
    rows = out_len // count
    tiles = k_all // LANES
    templates2 = jnp.transpose(templates, (1, 0, 2))
    both = local_corr(valid, waveform, templates2, moveouts.T, count)
    mine = halving_reduce_scatter(both, "chan", (tiles // 2) * rows)
    corr = mine[: tiles * rows].reshape(tiles, rows, LANES)
    energy_all = mine[tiles * rows:tiles * rows + out_len // LANES].reshape(out_len)
    block = count - 1 - lax.axis_index("chan")
    energy = lax.dynamic_slice_in_dim(energy_all, block * rows, rows)
    scale = jnp.sqrt(energy + 1e-06)
    best = jnp.max(corr / scale[None, :, None], axis=(0, 2))
    return jnp.flip(best, axis=0)


def solution(mesh):
    placed = (P("chan", "win"), P(None, "chan", None), P(None, "chan"), P("chan"))
    return jax.shard_map(
        on_device, mesh=mesh, in_specs=placed, out_specs=P(("win", "chan")), check_vma=False
    )
```

```python
import functools

import jax
import jax.numpy as jnp
from jax import lax
from jax.experimental import pallas as pl
from jax.experimental.pallas import tpu as pltpu
from jax.sharding import PartitionSpec as P

MAXSHIFT = 128
LANES = 128


def place_block(tr, mrow):
    rows, cols = tr.shape
    x = jnp.concatenate([tr, jnp.zeros((8, cols), tr.dtype)], axis=0)
    for level in range(3):
        amount = 1 << level
        moved = pltpu.roll(x, amount, 0)
        x = jnp.where((mrow >> level) & 1 == 1, moved, x)
    for level in range(3, (MAXSHIFT - 1).bit_length()):
        if level == 4:
            x = x.astype(jnp.bfloat16)
        pad = jnp.zeros((1 << level, cols), x.dtype)
        x = jnp.where(
            (mrow >> level) & 1 == 1,
            jnp.concatenate([pad, x], axis=0),
            jnp.concatenate([x, pad], axis=0),
        )
    return x


def corr_kernel(count, k_start, first, *refs):
    if first:
        valid_ref, w_ref, t_hbm, m_ref, out_ref, h_ref, p_scr, t_buf, tr_scr, sems = refs
    else:
        h_ref, t_hbm, m_ref, out_ref, p_scr, t_buf, tr_scr, sems = refs
    nc, k_all, length = t_buf.shape
    width = length + MAXSHIFT
    out_len = h_ref.shape[0]
    span = out_len + width
    copies = []
    for c in range(nc):
        copy = pltpu.make_async_copy(t_hbm.at[c, pl.ds(k_start, k_all)], t_buf.at[c], sems.at[c])
        copy.start()
        copies.append(copy)
    rows = out_len // count
    brows = out_ref.shape[0] // count
    corr_rows = (k_all // LANES) * rows
    if first:
        q = jnp.zeros((1, span), jnp.float32)
        for c in range(nc):
            row = w_ref[pl.ds(c, 1), :].astype(jnp.float32)
            row = jnp.where(valid_ref[c] == 1, row, 0.0)
            q = q + row * row
            a = pltpu.roll(jnp.broadcast_to(row, (out_len, span)), 1, 1, stride=1, stride_axis=0)
            h_ref[:, c * width:(c + 1) * width] = a[:, span - width:].astype(jnp.bfloat16)
        aq = pltpu.roll(jnp.broadcast_to(q, (out_len, span)), 1, 1, stride=1, stride_axis=0)
        energy = jnp.sum(aq[:, span - width:], axis=1, keepdims=True)
        energy_row = jnp.transpose(jnp.broadcast_to(energy, (out_len, LANES)))[0:1, :]
        tail = [energy_row[:, i:i + LANES] for i in range(0, out_len, LANES)]
        tail.append(jnp.zeros((brows - corr_rows - len(tail), LANES), jnp.float32))
        tail = jnp.concatenate(tail, axis=0)
        for b in range(count):
            out_ref[b * brows + corr_rows:(b + 1) * brows, :] = tail

    ri = lax.broadcasted_iota(jnp.int32, (length, length), 0)
    ci = lax.broadcasted_iota(jnp.int32, (length, length), 1)
    eye = jnp.where(ri == ci, 1.0, 0.0).astype(jnp.bfloat16)
    for c in range(nc):
        copies[c].wait()
        tr_scr[...] = lax.dot_general(
            eye, t_buf[c], (((1,), (1,)), ((), ())), preferred_element_type=jnp.float32
        )

        def body(kc, carry):
            k0 = pl.multiple_of(kc * LANES, LANES)
            tr = tr_scr[:, pl.ds(k0, LANES)]
            mrow = m_ref[pl.ds(c, 1), pl.ds(k0 + k_start, LANES)]
            x = place_block(tr, mrow)
            p_scr[pl.ds(c * width, width), pl.ds(k0, LANES)] = x
            return carry

        lax.fori_loop(0, k_all // LANES, body, 0)
    step = min(256, k_all)
    for n0 in range(0, k_all, step):
        res = jnp.dot(h_ref[...], p_scr[:, n0:n0 + step], preferred_element_type=jnp.float32)
        for sub in range(step // LANES):
            kt = n0 // LANES + sub
            for b in range(count):
                out_ref[b * brows + kt * rows:b * brows + (kt + 1) * rows, :] = res[
                    b * rows:(b + 1) * rows, sub * LANES:(sub + 1) * LANES
                ]


def local_corr(first, operands, templates2, count, k_start, k_all, out_len):
    nc, _, length = templates2.shape
    width = length + MAXSHIFT
    brows = (k_all // LANES) * (out_len // count) + (8 if first else 0)
    vmem = pl.BlockSpec(memory_space=pltpu.VMEM)
    out_shape = [jax.ShapeDtypeStruct((count * brows, LANES), jnp.float32)]
    if first:
        in_specs = [pl.BlockSpec(memory_space=pltpu.SMEM), vmem, pl.BlockSpec(memory_space=pl.ANY), vmem]
        out_shape.append(jax.ShapeDtypeStruct((out_len, nc * width), jnp.bfloat16))
    else:
        in_specs = [vmem, pl.BlockSpec(memory_space=pl.ANY), vmem]
    return pl.pallas_call(
        functools.partial(corr_kernel, count, k_start, first),
        out_shape=tuple(out_shape),
        in_specs=in_specs,
        out_specs=tuple([vmem] * len(out_shape)),
        scratch_shapes=[
            pltpu.VMEM((nc * width, k_all), jnp.bfloat16),
            pltpu.VMEM((nc, k_all, length), jnp.bfloat16),
            pltpu.VMEM((length, k_all), jnp.float32),
            pltpu.SemaphoreType.DMA((nc,)),
        ],
        compiler_params=pltpu.CompilerParams(vmem_limit_bytes=48 * 1024 * 1024),
        cost_estimate=pl.CostEstimate(
            flops=2 * out_len * nc * width * k_all,
            bytes_accessed=nc * k_all * length * 2 + count * brows * LANES * 4,
            transcendentals=0,
        ),
    )(*operands)


def halving_steps(blocks, me, bits, axis, count, remaining):
    remaining = list(remaining)
    for bit in bits:
        pos = remaining.index(bit)
        mine = (me >> bit) & 1
        keep = lax.dynamic_index_in_dim(blocks, mine, axis=pos, keepdims=False)
        send = lax.dynamic_index_in_dim(blocks, 1 - mine, axis=pos, keepdims=False)
        perm = [(j, j ^ (1 << bit)) for j in range(count)]
        blocks = keep + lax.ppermute(send, axis, perm)
        remaining.pop(pos)
    return blocks


def exchange(blocks, me, bit, axis, count, remaining):
    pos = remaining.index(bit)
    mine = (me >> bit) & 1
    keep = lax.dynamic_index_in_dim(blocks, mine, axis=pos, keepdims=False)
    send = lax.dynamic_index_in_dim(blocks, 1 - mine, axis=pos, keepdims=False)
    return keep, send, [(j, j ^ (1 << bit)) for j in range(count)]


def on_device(waveform, templates, moveouts, valid):
    k_all = templates.shape[0]
    count = lax.axis_size("chan")
    out_len = waveform.shape[1] - templates.shape[2] - MAXSHIFT
    rows = out_len // count
    tiles = k_all // LANES
    templates2 = jnp.transpose(templates, (1, 0, 2))
    mt = moveouts.T
    half = (tiles // 2) * LANES
    nbits = count.bit_length() - 1
    first, hankel = local_corr(
        True, (valid, waveform, templates2, mt), templates2, count, 0, half, out_len
    )
    if count & (count - 1) or nbits < 3 or half == 0:
        (second,) = local_corr(
            False, (hankel, templates2, mt), templates2, count, half, k_all - half, out_len
        )
        both = [first, second]
        if count & (count - 1):
            outs = []
            for x in both:
                brows = x.shape[0] // count
                flipped = jnp.flip(x.reshape(count, brows, LANES), 0).reshape(x.shape)
                outs.append(lax.psum_scatter(flipped, "chan", scatter_dimension=0, tiled=True))
            mine_first, mine_second = outs
        else:
            me = count - 1 - lax.axis_index("chan")
            every = list(range(nbits - 1, -1, -1))
            mine_first, mine_second = [
                halving_steps(
                    x.reshape((2,) * nbits + (x.shape[0] // count, LANES)),
                    me, list(range(nbits)), "chan", count, every,
                )
                for x in both
            ]
    else:
        me = count - 1 - lax.axis_index("chan")
        every = list(range(nbits - 1, -1, -1))
        rest = every[:-1]
        blocks_a = first.reshape((2,) * nbits + (first.shape[0] // count, LANES))
        keep_a, send_a, perm = exchange(blocks_a, me, 0, "chan", count, every)
        keep_a, send_a, hankel = lax.optimization_barrier((keep_a, send_a, hankel))
        got_a = lax.ppermute(send_a, "chan", perm)
        (second,) = local_corr(
            False, (hankel, templates2, mt), templates2, count, half, k_all - half, out_len
        )
        got_a, second = lax.optimization_barrier((got_a, second))
        a = halving_steps(keep_a + got_a, me, [1, 2], "chan", count, rest)
        blocks_b = second.reshape((2,) * nbits + (second.shape[0] // count, LANES))
        b = halving_steps(blocks_b, me, [0, 2, 1], "chan", count, every)
        joined = jnp.concatenate([b, a], axis=-2)
        joined = halving_steps(joined, me, list(range(3, nbits)), "chan", count, rest[:-2])
        split = b.shape[-2]
        mine_first, mine_second = joined[split:], joined[:split]
    first_tiles = half // LANES
    corr = jnp.concatenate(
        [mine_first[: first_tiles * rows], mine_second], axis=0
    ).reshape(tiles, rows, LANES)
    energy_all = mine_first[first_tiles * rows:first_tiles * rows + out_len // LANES]
    energy_all = energy_all.reshape(out_len)
    block = count - 1 - lax.axis_index("chan")
    energy = lax.dynamic_slice_in_dim(energy_all, block * rows, rows)
    scale = jnp.sqrt(energy + 1e-06)
    best = jnp.max(corr / scale[None, :, None], axis=(0, 2))
    return jnp.flip(best, axis=0)


def solution(mesh):
    placed = (P("chan", "win"), P(None, "chan", None), P(None, "chan"), P("chan"))
    return jax.shard_map(
        on_device, mesh=mesh, in_specs=placed, out_specs=P(("win", "chan")), check_vma=False
    )
```

```python
import functools

import jax
import jax.numpy as jnp
from jax import lax
from jax.experimental import pallas as pl
from jax.experimental.pallas import tpu as pltpu
from jax.sharding import PartitionSpec as P

MAXSHIFT = 128
LANES = 128


def place_block(tr, mrow):
    rows, cols = tr.shape
    x = jnp.concatenate([tr, jnp.zeros((8, cols), tr.dtype)], axis=0)
    for level in range(3):
        amount = 1 << level
        moved = pltpu.roll(x, amount, 0)
        x = jnp.where((mrow >> level) & 1 == 1, moved, x)
    for level in range(3, (MAXSHIFT - 1).bit_length()):
        if level == 4:
            x = x.astype(jnp.bfloat16)
        pad = jnp.zeros((1 << level, cols), x.dtype)
        x = jnp.where(
            (mrow >> level) & 1 == 1,
            jnp.concatenate([pad, x], axis=0),
            jnp.concatenate([x, pad], axis=0),
        )
    return x


def corr_kernel(count, valid_ref, w_ref, t_hbm, m_ref, out_ref, h_scr, p_scr, t_buf, tr_scr, sems):
    nc, span = w_ref.shape
    k_all = t_hbm.shape[1]
    length = t_hbm.shape[2]
    width = length + MAXSHIFT
    out_len = span - width
    copies = []
    for c in range(nc):
        copy = pltpu.make_async_copy(
            t_hbm.at[c], t_buf.at[c], sems.at[c]
        )
        copy.start()
        copies.append(copy)
    q = jnp.zeros((1, span), jnp.float32)
    for c in range(nc):
        row = w_ref[pl.ds(c, 1), :].astype(jnp.float32)
        row = jnp.where(valid_ref[c] == 1, row, 0.0)
        q = q + row * row
        a = pltpu.roll(jnp.broadcast_to(row, (out_len, span)), 1, 1, stride=1, stride_axis=0)
        h_scr[:, c * width:(c + 1) * width] = a[:, span - width:].astype(jnp.bfloat16)
    aq = pltpu.roll(jnp.broadcast_to(q, (out_len, span)), 1, 1, stride=1, stride_axis=0)
    energy = jnp.sum(aq[:, span - width:], axis=1, keepdims=True)
    rows = out_len // count
    brows = out_ref.shape[0] // count
    corr_rows = (k_all // LANES) * rows
    energy_row = jnp.transpose(jnp.broadcast_to(energy, (out_len, LANES)))[0:1, :]
    tail = [energy_row[:, i:i + LANES] for i in range(0, out_len, LANES)]
    tail.append(jnp.zeros((brows - corr_rows - len(tail), LANES), jnp.float32))
    tail = jnp.concatenate(tail, axis=0)
    for b in range(count):
        out_ref[b * brows + corr_rows:(b + 1) * brows, :] = tail

    ri = lax.broadcasted_iota(jnp.int32, (length, length), 0)
    ci = lax.broadcasted_iota(jnp.int32, (length, length), 1)
    eye = jnp.where(ri == ci, 1.0, 0.0).astype(jnp.bfloat16)
    for c in range(nc):
        copies[c].wait()
        tr_scr[...] = lax.dot_general(
            eye, t_buf[c], (((1,), (1,)), ((), ())), preferred_element_type=jnp.float32
        )

        def body(kc, carry):
            k0 = pl.multiple_of(kc * LANES, LANES)
            tr = tr_scr[:, pl.ds(k0, LANES)]
            mrow = m_ref[pl.ds(c, 1), pl.ds(k0, LANES)]
            x = place_block(tr, mrow)
            p_scr[pl.ds(c * width, width), pl.ds(k0, LANES)] = x
            return carry

        lax.fori_loop(0, k_all // LANES, body, 0)
    step = 256
    for n0 in range(0, k_all, step):
        res = jnp.dot(h_scr[...], p_scr[:, n0:n0 + step], preferred_element_type=jnp.float32)
        for sub in range(step // LANES):
            kt = n0 // LANES + sub
            for b in range(count):
                out_ref[b * brows + kt * rows:b * brows + (kt + 1) * rows, :] = res[
                    b * rows:(b + 1) * rows, sub * LANES:(sub + 1) * LANES
                ]


def local_corr(valid, waveform, templates2, mt, count):
    nc, span = waveform.shape
    k_all = templates2.shape[1]
    length = templates2.shape[2]
    width = length + MAXSHIFT
    out_len = span - width
    brows = (k_all // LANES) * (out_len // count) + 8
    return pl.pallas_call(
        functools.partial(corr_kernel, count),
        out_shape=jax.ShapeDtypeStruct((count * brows, LANES), jnp.float32),
        in_specs=[
            pl.BlockSpec(memory_space=pltpu.SMEM),
            pl.BlockSpec(memory_space=pltpu.VMEM),
            pl.BlockSpec(memory_space=pl.ANY),
            pl.BlockSpec(memory_space=pltpu.VMEM),
        ],
        out_specs=pl.BlockSpec(memory_space=pltpu.VMEM),
        scratch_shapes=[
            pltpu.VMEM((out_len, nc * width), jnp.bfloat16),
            pltpu.VMEM((nc * width, k_all), jnp.bfloat16),
            pltpu.VMEM((nc, k_all, length), jnp.bfloat16),
            pltpu.VMEM((length, k_all), jnp.float32),
            pltpu.SemaphoreType.DMA((nc,)),
        ],
        compiler_params=pltpu.CompilerParams(vmem_limit_bytes=48 * 1024 * 1024),
        cost_estimate=pl.CostEstimate(
            flops=2 * out_len * nc * width * k_all,
            bytes_accessed=templates2.size * 2 + out_len * (k_all + LANES) * 4,
            transcendentals=0,
        ),
    )(valid, waveform, templates2, mt)


def halving_steps(blocks, me, bits, axis, count, remaining):
    remaining = list(remaining)
    for bit in bits:
        pos = remaining.index(bit)
        mine = (me >> bit) & 1
        keep = lax.dynamic_index_in_dim(blocks, mine, axis=pos, keepdims=False)
        send = lax.dynamic_index_in_dim(blocks, 1 - mine, axis=pos, keepdims=False)
        perm = [(j, j ^ (1 << bit)) for j in range(count)]
        blocks = keep + lax.ppermute(send, axis, perm)
        remaining.pop(pos)
    return blocks


def halving_reduce_scatter(x, axis, split):
    count = lax.axis_size(axis)
    brows = x.shape[0] // count
    if count & (count - 1):
        flipped = jnp.flip(x.reshape(count, brows, LANES), 0).reshape(x.shape)
        return lax.psum_scatter(flipped, axis, scatter_dimension=0, tiled=True)
    me = count - 1 - lax.axis_index(axis)
    nbits = count.bit_length() - 1
    blocks = x.reshape((2,) * nbits + (brows, LANES))
    every = list(range(nbits - 1, -1, -1))
    if nbits < 3:
        return halving_steps(blocks, me, list(range(nbits)), axis, count, every)
    first = halving_steps(blocks[..., :split, :], me, [0, 1, 2], axis, count, every)
    second = halving_steps(blocks[..., split:, :], me, [0, 2, 1], axis, count, every)
    joined = jnp.concatenate([first, second], axis=-2)
    return halving_steps(joined, me, list(range(3, nbits)), axis, count, every[:-3])


def on_device(waveform, templates, moveouts, valid):
    k_all = templates.shape[0]
    count = lax.axis_size("chan")
    out_len = waveform.shape[1] - templates.shape[2] - MAXSHIFT
    rows = out_len // count
    tiles = k_all // LANES
    templates2 = jnp.transpose(templates, (1, 0, 2))
    both = local_corr(valid, waveform, templates2, moveouts.T, count)
    mine = halving_reduce_scatter(both, "chan", (tiles // 2) * rows)
    corr = mine[: tiles * rows].reshape(tiles, rows, LANES)
    energy_all = mine[tiles * rows:tiles * rows + out_len // LANES].reshape(out_len)
    block = count - 1 - lax.axis_index("chan")
    energy = lax.dynamic_slice_in_dim(energy_all, block * rows, rows)
    scale = jnp.sqrt(energy + 1e-06)
    best = jnp.max(corr / scale[None, :, None], axis=(0, 2))
    return jnp.flip(best, axis=0)


def solution(mesh):
    placed = (P("chan", "win"), P(None, "chan", None), P(None, "chan"), P("chan"))
    return jax.shard_map(
        on_device, mesh=mesh, in_specs=placed, out_specs=P(("win", "chan")), check_vma=False
    )
```

```python
import functools

import jax
import jax.numpy as jnp
from jax import lax
from jax.experimental import pallas as pl
from jax.experimental.pallas import tpu as pltpu
from jax.sharding import PartitionSpec as P

MAXSHIFT = 128
LANES = 128


def place_block(tr, mrow):
    rows, cols = tr.shape
    x = jnp.concatenate([tr, jnp.zeros((8, cols), tr.dtype)], axis=0)
    for level in range(3):
        amount = 1 << level
        moved = pltpu.roll(x, amount, 0)
        x = jnp.where((mrow >> level) & 1 == 1, moved, x)
    for level in range(3, (MAXSHIFT - 1).bit_length()):
        if level == 4:
            x = x.astype(jnp.bfloat16)
        pad = jnp.zeros((1 << level, cols), x.dtype)
        x = jnp.where(
            (mrow >> level) & 1 == 1,
            jnp.concatenate([pad, x], axis=0),
            jnp.concatenate([x, pad], axis=0),
        )
    return x


def corr_kernel(count, valid_ref, w_ref, t_hbm, m_ref, out_ref, h_scr, p_scr, t_buf, tr_scr, sems):
    nc, span = w_ref.shape
    k_all = t_hbm.shape[1]
    length = t_hbm.shape[2]
    width = length + MAXSHIFT
    out_len = span - width
    copies = []
    for c in range(nc):
        copy = pltpu.make_async_copy(
            t_hbm.at[c], t_buf.at[c], sems.at[c]
        )
        copy.start()
        copies.append(copy)
    q = jnp.zeros((1, span), jnp.float32)
    for c in range(nc):
        row = w_ref[pl.ds(c, 1), :].astype(jnp.float32)
        row = jnp.where(valid_ref[c] == 1, row, 0.0)
        q = q + row * row
        a = pltpu.roll(jnp.broadcast_to(row, (out_len, span)), 1, 1, stride=1, stride_axis=0)
        h_scr[:, c * width:(c + 1) * width] = a[:, span - width:].astype(jnp.bfloat16)
    aq = pltpu.roll(jnp.broadcast_to(q, (out_len, span)), 1, 1, stride=1, stride_axis=0)
    energy = jnp.sum(aq[:, span - width:], axis=1, keepdims=True)
    rows = out_len // count
    brows = out_ref.shape[0] // count
    corr_rows = (k_all // LANES) * rows
    energy_row = jnp.transpose(jnp.broadcast_to(energy, (out_len, LANES)))[0:1, :]
    tail = [energy_row[:, i:i + LANES] for i in range(0, out_len, LANES)]
    tail.append(jnp.zeros((brows - corr_rows - len(tail), LANES), jnp.float32))
    tail = jnp.concatenate(tail, axis=0)
    for b in range(count):
        out_ref[b * brows + corr_rows:(b + 1) * brows, :] = tail

    ri = lax.broadcasted_iota(jnp.int32, (length, length), 0)
    ci = lax.broadcasted_iota(jnp.int32, (length, length), 1)
    eye = jnp.where(ri == ci, 1.0, 0.0).astype(jnp.bfloat16)
    for c in range(nc):
        copies[c].wait()
        tr_scr[...] = lax.dot_general(
            eye, t_buf[c], (((1,), (1,)), ((), ())), preferred_element_type=jnp.float32
        )

        def body(kc, carry):
            k0 = pl.multiple_of(kc * LANES, LANES)
            tr = tr_scr[:, pl.ds(k0, LANES)]
            mrow = m_ref[pl.ds(c, 1), pl.ds(k0, LANES)]
            x = place_block(tr, mrow)
            p_scr[pl.ds(c * width, width), pl.ds(k0, LANES)] = x
            return carry

        lax.fori_loop(0, k_all // LANES, body, 0)
    step = 256
    for n0 in range(0, k_all, step):
        res = jnp.dot(h_scr[...], p_scr[:, n0:n0 + step], preferred_element_type=jnp.float32)
        for sub in range(step // LANES):
            kt = n0 // LANES + sub
            for b in range(count):
                out_ref[b * brows + kt * rows:b * brows + (kt + 1) * rows, :] = res[
                    b * rows:(b + 1) * rows, sub * LANES:(sub + 1) * LANES
                ]


def local_corr(valid, waveform, templates2, mt, count):
    nc, span = waveform.shape
    k_all = templates2.shape[1]
    length = templates2.shape[2]
    width = length + MAXSHIFT
    out_len = span - width
    brows = (k_all // LANES) * (out_len // count) + 8
    return pl.pallas_call(
        functools.partial(corr_kernel, count),
        out_shape=jax.ShapeDtypeStruct((count * brows, LANES), jnp.float32),
        in_specs=[
            pl.BlockSpec(memory_space=pltpu.SMEM),
            pl.BlockSpec(memory_space=pltpu.VMEM),
            pl.BlockSpec(memory_space=pl.ANY),
            pl.BlockSpec(memory_space=pltpu.VMEM),
        ],
        out_specs=pl.BlockSpec(memory_space=pltpu.VMEM),
        scratch_shapes=[
            pltpu.VMEM((out_len, nc * width), jnp.bfloat16),
            pltpu.VMEM((nc * width, k_all), jnp.bfloat16),
            pltpu.VMEM((nc, k_all, length), jnp.bfloat16),
            pltpu.VMEM((length, k_all), jnp.float32),
            pltpu.SemaphoreType.DMA((nc,)),
        ],
        compiler_params=pltpu.CompilerParams(vmem_limit_bytes=48 * 1024 * 1024),
        cost_estimate=pl.CostEstimate(
            flops=2 * out_len * nc * width * k_all,
            bytes_accessed=templates2.size * 2 + out_len * (k_all + LANES) * 4,
            transcendentals=0,
        ),
    )(valid, waveform, templates2, mt)


def halving_steps(blocks, me, bits, axis, count, remaining):
    remaining = list(remaining)
    for bit in bits:
        pos = remaining.index(bit)
        mine = (me >> bit) & 1
        keep = lax.dynamic_index_in_dim(blocks, mine, axis=pos, keepdims=False)
        send = lax.dynamic_index_in_dim(blocks, 1 - mine, axis=pos, keepdims=False)
        perm = [(j, j ^ (1 << bit)) for j in range(count)]
        blocks = keep + lax.ppermute(send, axis, perm)
        remaining.pop(pos)
    return blocks


def halving_reduce_scatter(x, axis, split):
    count = lax.axis_size(axis)
    brows = x.shape[0] // count
    if count & (count - 1):
        flipped = jnp.flip(x.reshape(count, brows, LANES), 0).reshape(x.shape)
        return lax.psum_scatter(flipped, axis, scatter_dimension=0, tiled=True)
    me = count - 1 - lax.axis_index(axis)
    nbits = count.bit_length() - 1
    blocks = x.reshape((2,) * nbits + (brows, LANES))
    every = list(range(nbits - 1, -1, -1))
    if nbits < 3:
        return halving_steps(blocks, me, list(range(nbits)), axis, count, every)
    first = halving_steps(blocks[..., :split, :], me, [0, 1, 2], axis, count, every)
    second = halving_steps(blocks[..., split:, :], me, [0, 2, 1], axis, count, every)
    joined = jnp.concatenate([first, second], axis=-2)
    return halving_steps(joined, me, list(range(3, nbits)), axis, count, every[:-3])


def on_device(waveform, templates, moveouts, valid):
    k_all = templates.shape[0]
    count = lax.axis_size("chan")
    out_len = waveform.shape[1] - templates.shape[2] - MAXSHIFT
    rows = out_len // count
    tiles = k_all // LANES
    templates2 = jnp.transpose(templates, (1, 0, 2))
    both = local_corr(valid, waveform, templates2, moveouts.T, count)
    mine = halving_reduce_scatter(both, "chan", (tiles // 2) * rows)
    corr = mine[: tiles * rows].reshape(tiles, rows, LANES)
    energy_all = mine[tiles * rows:tiles * rows + out_len // LANES].reshape(out_len)
    block = count - 1 - lax.axis_index("chan")
    energy = lax.dynamic_slice_in_dim(energy_all, block * rows, rows)
    scale = jnp.sqrt(energy + 1e-06)
    best = jnp.max(corr, axis=(0, 2)) / scale
    return jnp.flip(best, axis=0)


def solution(mesh):
    placed = (P("chan", "win"), P(None, "chan", None), P(None, "chan"), P("chan"))
    return jax.shard_map(
        on_device, mesh=mesh, in_specs=placed, out_specs=P(("win", "chan")), check_vma=False
    )
```

```python
import functools

import jax
import jax.numpy as jnp
from jax import lax
from jax.experimental import pallas as pl
from jax.experimental.pallas import tpu as pltpu
from jax.sharding import PartitionSpec as P

MAXSHIFT = 128
LANES = 128


def place_block(tr, mrow):
    rows, cols = tr.shape
    x = jnp.concatenate([tr, jnp.zeros((8, cols), tr.dtype)], axis=0)
    for level in range(3):
        amount = 1 << level
        moved = pltpu.roll(x, amount, 0)
        x = jnp.where((mrow >> level) & 1 == 1, moved, x)
    for level in range(3, (MAXSHIFT - 1).bit_length()):
        if level == 4:
            x = x.astype(jnp.bfloat16)
        pad = jnp.zeros((1 << level, cols), x.dtype)
        x = jnp.where(
            (mrow >> level) & 1 == 1,
            jnp.concatenate([pad, x], axis=0),
            jnp.concatenate([x, pad], axis=0),
        )
    return x


def corr_kernel(count, pos_ref, valid_ref, w_ref, t_hbm, m_ref, out_ref, h_scr, p_scr, t_buf, tr_scr, sems):
    nc, span = w_ref.shape
    k_all = t_hbm.shape[1]
    length = t_hbm.shape[2]
    width = length + MAXSHIFT
    out_len = span - width
    copies = []
    for c in range(nc):
        copy = pltpu.make_async_copy(
            t_hbm.at[c], t_buf.at[c], sems.at[c]
        )
        copy.start()
        copies.append(copy)
    q = jnp.zeros((1, span), jnp.float32)
    for c in range(nc):
        row = w_ref[pl.ds(c, 1), :].astype(jnp.float32)
        row = jnp.where(valid_ref[c] == 1, row, 0.0)
        q = q + row * row
        a = pltpu.roll(jnp.broadcast_to(row, (out_len, span)), 1, 1, stride=1, stride_axis=0)
        h_scr[:, c * width:(c + 1) * width] = a[:, span - width:].astype(jnp.bfloat16)
    aq = pltpu.roll(jnp.broadcast_to(q, (out_len, span)), 1, 1, stride=1, stride_axis=0)
    energy = jnp.sum(aq[:, span - width:], axis=1, keepdims=True)
    rows = out_len // count
    brows = out_ref.shape[0] // count
    corr_rows = (k_all // LANES) * rows
    energy_row = jnp.transpose(jnp.broadcast_to(energy, (out_len, LANES)))[0:1, :]
    tail = [energy_row[:, i:i + LANES] for i in range(0, out_len, LANES)]
    tail.append(jnp.zeros((brows - corr_rows - len(tail), LANES), jnp.float32))
    tail = jnp.concatenate(tail, axis=0)
    for b in range(count):
        out_ref[b * brows + corr_rows:(b + 1) * brows, :] = tail

    ri = lax.broadcasted_iota(jnp.int32, (length, length), 0)
    ci = lax.broadcasted_iota(jnp.int32, (length, length), 1)
    eye = jnp.where(ri == ci, 1.0, 0.0).astype(jnp.bfloat16)
    for c in range(nc):
        copies[c].wait()
        tr_scr[...] = lax.dot_general(
            eye, t_buf[c], (((1,), (1,)), ((), ())), preferred_element_type=jnp.float32
        )

        def body(kc, carry):
            k0 = pl.multiple_of(kc * LANES, LANES)
            tr = tr_scr[:, pl.ds(k0, LANES)]
            mrow = m_ref[pl.ds(c, 1), pl.ds(k0, LANES)]
            x = place_block(tr, mrow)
            p_scr[pl.ds(c * width, width), pl.ds(k0, LANES)] = x
            return carry

        lax.fori_loop(0, k_all // LANES, body, 0)
    step = 256
    for n0 in range(0, k_all, step):
        res = jnp.dot(h_scr[...], p_scr[:, n0:n0 + step], preferred_element_type=jnp.float32)
        for sub in range(step // LANES):
            kt = n0 // LANES + sub
            for b in range(count):
                start = pl.multiple_of((b ^ pos_ref[0]) * brows + kt * rows, rows)
                out_ref[pl.ds(start, rows), :] = res[
                    b * rows:(b + 1) * rows, sub * LANES:(sub + 1) * LANES
                ]


def local_corr(pos, valid, waveform, templates2, mt, count):
    nc, span = waveform.shape
    k_all = templates2.shape[1]
    length = templates2.shape[2]
    width = length + MAXSHIFT
    out_len = span - width
    brows = (k_all // LANES) * (out_len // count) + 8
    return pl.pallas_call(
        functools.partial(corr_kernel, count),
        out_shape=jax.ShapeDtypeStruct((count * brows, LANES), jnp.float32),
        in_specs=[
            pl.BlockSpec(memory_space=pltpu.SMEM),
            pl.BlockSpec(memory_space=pltpu.SMEM),
            pl.BlockSpec(memory_space=pltpu.VMEM),
            pl.BlockSpec(memory_space=pl.ANY),
            pl.BlockSpec(memory_space=pltpu.VMEM),
        ],
        out_specs=pl.BlockSpec(memory_space=pltpu.VMEM),
        scratch_shapes=[
            pltpu.VMEM((out_len, nc * width), jnp.bfloat16),
            pltpu.VMEM((nc * width, k_all), jnp.bfloat16),
            pltpu.VMEM((nc, k_all, length), jnp.bfloat16),
            pltpu.VMEM((length, k_all), jnp.float32),
            pltpu.SemaphoreType.DMA((nc,)),
        ],
        compiler_params=pltpu.CompilerParams(vmem_limit_bytes=48 * 1024 * 1024),
        cost_estimate=pl.CostEstimate(
            flops=2 * out_len * nc * width * k_all,
            bytes_accessed=templates2.size * 2 + out_len * (k_all + LANES) * 4,
            transcendentals=0,
        ),
    )(pos, valid, waveform, templates2, mt)


def halving_steps(blocks, me, bits, axis, count, remaining, relabeled=True):
    remaining = list(remaining)
    for bit in bits:
        pos = remaining.index(bit)
        mine = (me >> bit) & 1
        if relabeled:
            keep = lax.index_in_dim(blocks, 0, axis=pos, keepdims=False)
            send = lax.index_in_dim(blocks, 1, axis=pos, keepdims=False)
        else:
            keep = lax.dynamic_index_in_dim(blocks, mine, axis=pos, keepdims=False)
            send = lax.dynamic_index_in_dim(blocks, 1 - mine, axis=pos, keepdims=False)
        perm = [(j, j ^ (1 << bit)) for j in range(count)]
        blocks = keep + lax.ppermute(send, axis, perm)
        remaining.pop(pos)
    return blocks


def halving_reduce_scatter(x, axis, split):
    count = lax.axis_size(axis)
    brows = x.shape[0] // count
    if count & (count - 1):
        flipped = jnp.flip(x.reshape(count, brows, LANES), 0).reshape(x.shape)
        return lax.psum_scatter(flipped, axis, scatter_dimension=0, tiled=True)
    me = count - 1 - lax.axis_index(axis)
    nbits = count.bit_length() - 1
    blocks = x.reshape((2,) * nbits + (brows, LANES))
    every = list(range(nbits - 1, -1, -1))
    if nbits < 3:
        return halving_steps(blocks, me, list(range(nbits)), axis, count, every)
    first = halving_steps(blocks[..., :split, :], me, [0, 1, 2], axis, count, every)
    second = halving_steps(blocks[..., split:, :], me, [0, 2, 1], axis, count, every)
    joined = jnp.concatenate([first, second], axis=-2)
    return halving_steps(joined, me, list(range(3, nbits)), axis, count, every[:-3])


def on_device(waveform, templates, moveouts, valid):
    k_all = templates.shape[0]
    count = lax.axis_size("chan")
    out_len = waveform.shape[1] - templates.shape[2] - MAXSHIFT
    rows = out_len // count
    tiles = k_all // LANES
    templates2 = jnp.transpose(templates, (1, 0, 2))
    power_of_two = count & (count - 1) == 0
    pos = (count - 1 - lax.axis_index("chan")) if power_of_two else 0
    pos = jnp.full((1,), pos, jnp.int32)
    both = local_corr(pos, valid, waveform, templates2, moveouts.T, count)
    mine = halving_reduce_scatter(both, "chan", (tiles // 2) * rows)
    corr = mine[: tiles * rows].reshape(tiles, rows, LANES)
    energy_all = mine[tiles * rows:tiles * rows + out_len // LANES].reshape(out_len)
    block = count - 1 - lax.axis_index("chan")
    energy = lax.dynamic_slice_in_dim(energy_all, block * rows, rows)
    scale = jnp.sqrt(energy + 1e-06)
    best = jnp.max(corr, axis=(0, 2)) / scale
    return jnp.flip(best, axis=0)


def solution(mesh):
    placed = (P("chan", "win"), P(None, "chan", None), P(None, "chan"), P("chan"))
    return jax.shard_map(
        on_device, mesh=mesh, in_specs=placed, out_specs=P(("win", "chan")), check_vma=False
    )
```
